256 devices in a mesh: act: 32 (over x, y, core), pix: 8 (over z).
Axes of the slice: x: 4, y: 4, z: 8, core: 2. Of those that a mesh axis runs over, the one named last changes fastest.
Arguments:
- pixel_index: int32 [8, 512], P('pix'), may hold values from 0 to 65535
- act_map: int32 [32768], P('act'), may hold values from 0 to 32767, each once
- omega: bfloat16 [32768, 128], P('act'), may hold values from -6 to 6
- pupil_field: float32 [8, 2, 32768], P('pix', None, 'act'), may hold values from -6 to 6
- channel_scale: float32 [8], P('pix'), may hold values from 0.9 to 1.1
- channel_flux: float32 [8], P('pix'), may hold values from 0.3 to 3
Outputs:
- basis_out: float32 [8, 1024, 128], P('pix', 'act')
- projection: float32 [128, 32768], P('pix', 'act')
- r_factor: float32 [128, 128], replicated
The draws below stay inside these ranges and needn't reach their ends.
Inputs may be any that keep to these rules, and one draw needn't show every extreme that they name: `act_map`: every number of 0 to 32767 appears once. `pixel_index`: pixels of a channel may repeat.
All inputs are finite; a program needn't handle non-finite values.
Results may differ from the reference program's by a relative error of at most 0.0048.
Values may be sent and summed in bfloat16 or wider, within the bound.
No kernel may reach another device: no remote copies, remote signals or barrier semaphores. Data moves between devices by JAX's collectives and lax.ppermute only.
A program may use at most 64 MiB of HBM per device.

```python
import math
import jax
import jax.numpy as jnp
from jax import lax

GRID = 128
FOCAL = 256
RANK = 128
PIX = 512
ACT = 32768
CHANNELS = 8
ROWS = 8192


def place_ends(array, stream_key, smallest, top_value):
    spot = [jax.random.randint(jax.random.fold_in(stream_key, axis), (), 0, length) for axis, length in enumerate(array.shape)]
    main_axis = array.shape.index(max(array.shape))
    beside = spot[:main_axis] + [(spot[main_axis] + 1) % array.shape[main_axis]] + spot[main_axis + 1:]
    return array.at[tuple(spot)].set(smallest).at[tuple(beside)].set(top_value)


def steps_of(key, dims, split, low, high):
    factor_of = 1.0
    for position, blocks in split:
        steps = jax.random.uniform(jax.random.fold_in(jax.random.fold_in(key, 6), position), (blocks,), jnp.float32, low / len(split), high / len(split))
        factor_of = factor_of * jnp.repeat(jnp.exp(steps), dims[position] // blocks).reshape((-1,) + (1,) * (len(dims) - 1 - position))
    return factor_of


def noise(rng, extent, scale, most, split=(), kind=jnp.bfloat16):
    array = jax.random.normal(rng, extent, jnp.float32) * scale
    if len(split) > 0:
        array = steps_of(rng, extent, split, -0.22, 0.18) * array
    return jnp.clip(array, min=-most, max=most).astype(kind)


def setup_inputs(seed: int = 0) -> dict:
    key_list = jax.random.split(jax.random.key(seed), 7)
    pixel_index = place_ends(jax.random.randint(key_list[0], (CHANNELS, PIX), 0, FOCAL * FOCAL), jax.random.fold_in(key_list[0], 1), 0, (FOCAL * FOCAL) - 1).astype(jnp.int32)
    act_map = jax.random.permutation(key_list[1], ACT).astype(jnp.int32)
    omega = noise(key_list[2], (ACT, RANK), 1.0, 6.0, ((0, 32),))
    pupil_field = noise(key_list[3], (CHANNELS, 2, ACT), 1.0, 6.0, ((0, 8), (2, 32)), jnp.float32)
    channel_scale = jnp.clip(0.9 + 0.20000005 * jax.random.uniform(key_list[4], (CHANNELS,), jnp.float32) ** steps_of(key_list[4], (CHANNELS,), ((0, 8),), -0.2, 0.2), 0.9, 1.1)
    channel_flux = jnp.clip(jnp.exp(math.log(3.0) - 2.3025851 * jax.random.uniform(key_list[5], (CHANNELS,), jnp.float32) ** steps_of(key_list[5], (CHANNELS,), ((0, 8),), -0.2, 0.2)), 0.3, 3.0)
    return dict(pixel_index=pixel_index, act_map=act_map, omega=omega, pupil_field=pupil_field, channel_scale=channel_scale, channel_flux=channel_flux)


TWO_PI = 2.0 * math.pi
INFL_RATE = 4.5
DEFOCUS_RATE = 6.0

def jacobian_rows(pixels, wave_scale, flux_level, codes, field_re, field_im):
    delta_u = pixels // FOCAL - FOCAL // 2
    delta_v = pixels % FOCAL - FOCAL // 2
    mirror = codes // (GRID * GRID)
    column_x = codes // GRID % GRID - GRID // 2
    column_y = codes % GRID - GRID // 2
    phase_int = delta_u[:, None] * column_x[None, :] + delta_v[:, None] * column_y[None, :]
    radius = (delta_u * delta_u + delta_v * delta_v).astype(jnp.float32)
    amplitude = flux_level * jnp.exp(-INFL_RATE * radius / (FOCAL * FOCAL))
    defocus = radius * (TWO_PI * DEFOCUS_RATE / (FOCAL * FOCAL)) / wave_scale
    phase_angle = mirror.astype(jnp.float32)[None, :] * defocus[:, None] - TWO_PI / FOCAL * wave_scale * phase_int.astype(jnp.float32)
    cosine = jnp.cos(phase_angle)
    sine_part = jnp.sin(phase_angle)
    real_part = amplitude[:, None] * (field_re[None, :] * cosine - field_im[None, :] * sine_part)
    imag_part = amplitude[:, None] * (field_re[None, :] * sine_part + field_im[None, :] * cosine)
    stacked = jnp.stack([real_part, imag_part], axis=1)
    return stacked.reshape(2 * pixels.shape[0], codes.shape[0]).astype(jnp.bfloat16)

def reference(pixel_index, act_map, omega, pupil_field, channel_scale, channel_flux):
    block_cols = min(1024, ACT)
    block_count = ACT // block_cols
    codes_b = act_map.reshape(block_count, block_cols)
    omega_b = omega.reshape(block_count, block_cols, RANK)
    field_b = pupil_field.reshape(CHANNELS, 2, block_count, block_cols)

    def channel_block(chan_id, block_id):
        return jacobian_rows(pixel_index[chan_id], channel_scale[chan_id], channel_flux[chan_id], codes_b[block_id], field_b[chan_id, 0, block_id], field_b[chan_id, 1, block_id])

    def channel_sketch(chan_id):

        def add_block(accum_sum, block_id):
            jacobian = channel_block(chan_id, block_id)
            return (accum_sum + jnp.dot(jacobian.astype(jnp.float32), omega_b[block_id].astype(jnp.float32), preferred_element_type=jnp.float32), None)
        accum_sum, unused = lax.scan(add_block, jnp.zeros((2 * PIX, RANK), jnp.float32), jnp.arange(block_count, dtype=jnp.int32))
        return accum_sum
    sketch = lax.map(channel_sketch, jnp.arange(CHANNELS, dtype=jnp.int32)).reshape(ROWS, RANK)
    gram_matrix = lax.dot_general(sketch.astype(jnp.float32), sketch.astype(jnp.float32), (((0,), (0,)), ((), ())), precision=lax.Precision.HIGHEST, preferred_element_type=jnp.float32)
    lower_factor = jnp.linalg.cholesky(gram_matrix)
    basis = jax.scipy.linalg.solve_triangular(lower_factor, sketch.T, lower=True).T
    coarse = basis.astype(jnp.bfloat16).reshape(CHANNELS, 2 * PIX, RANK)

    def block_projection(block_id):

        def add_channel(accum_sum, chan_id):
            jacobian = channel_block(chan_id, block_id)
            term = lax.dot_general(coarse[chan_id].astype(jnp.float32), jacobian.astype(jnp.float32), (((0,), (0,)), ((), ())), preferred_element_type=jnp.float32)
            return (accum_sum + term, None)
        accum_sum, unused = lax.scan(add_channel, jnp.zeros((RANK, block_cols), jnp.float32), jnp.arange(CHANNELS, dtype=jnp.int32))
        return accum_sum
    blocks = lax.map(block_projection, jnp.arange(block_count, dtype=jnp.int32))
    projection = jnp.transpose(blocks, (1, 0, 2)).reshape(RANK, ACT)
    basis_out = (basis * math.sqrt(ROWS)).reshape(CHANNELS, 2 * PIX, RANK)
    r_factor = lower_factor.T / math.sqrt(ROWS * ACT)
    return (basis_out, projection, r_factor)
```

```python
import math

import jax
import jax.numpy as jnp
from jax import lax
from jax.sharding import PartitionSpec as P

GRID = 128
FOCAL = 256
RANK = 128
ACT = 32768


TWO_PI = 2.0 * math.pi
INFL_RATE = 4.5
DEFOCUS_RATE = 6.0


def jacobian_planes(pixels, wave_scale, flux_level, codes, field_re, field_im):
    delta_u = pixels // FOCAL - FOCAL // 2
    delta_v = pixels % FOCAL - FOCAL // 2
    mirror = codes // (GRID * GRID)
    column_x = codes // GRID % GRID - GRID // 2
    column_y = codes % GRID - GRID // 2
    phase_int = delta_u[:, None] * column_x[None, :] + delta_v[:, None] * column_y[None, :]
    radius = (delta_u * delta_u + delta_v * delta_v).astype(jnp.float32)
    amplitude = flux_level * jnp.exp(-INFL_RATE * radius / (FOCAL * FOCAL))
    defocus = radius * (TWO_PI * DEFOCUS_RATE / (FOCAL * FOCAL)) / wave_scale
    phase_angle = mirror.astype(jnp.float32)[None, :] * defocus[
        :, None
    ] - TWO_PI / FOCAL * wave_scale * phase_int.astype(jnp.float32)
    cosine = jnp.cos(phase_angle)
    sine_part = jnp.sin(phase_angle)
    real_part = amplitude[:, None] * (field_re[None, :] * cosine - field_im[None, :] * sine_part)
    imag_part = amplitude[:, None] * (field_re[None, :] * sine_part + field_im[None, :] * cosine)
    return real_part.astype(jnp.bfloat16), imag_part.astype(jnp.bfloat16)


def gram_of(sketch):
    return lax.dot_general(
        sketch,
        sketch,
        (((0,), (0,)), ((), ())),
        precision=lax.Precision.HIGHEST,
        preferred_element_type=jnp.float32,
    )


def on_device(pixel_index, act_map, omega, pupil_field, channel_scale, channel_flux):
    pixels = pixel_index[0]
    npix = pixels.shape[0]
    rows_dev = 2 * npix
    act_count = lax.axis_size("act")
    pix_count = lax.axis_size("pix")
    total_rows = rows_dev * pix_count
    share_pix = npix // act_count
    real_rows, imag_rows = jacobian_planes(
        pixels, channel_scale[0], channel_flux[0], act_map, pupil_field[0, 0], pupil_field[0, 1]
    )
    jac = jnp.concatenate([real_rows, imag_rows], axis=0)
    partial_sketch = jnp.dot(jac, omega, preferred_element_type=jnp.float32)
    sketch = lax.psum(partial_sketch, "act")
    gram_matrix = lax.psum(gram_of(sketch), "pix")
    lower_factor = jnp.linalg.cholesky(gram_matrix)
    basis = jax.scipy.linalg.solve_triangular(lower_factor, sketch.T, lower=True).T
    first = lax.axis_index("act") * share_pix
    own_re = lax.dynamic_slice_in_dim(basis, first, share_pix, 0)
    own_im = lax.dynamic_slice_in_dim(basis, npix + first, share_pix, 0)
    own_basis = jnp.stack([own_re, own_im], axis=1).reshape(2 * share_pix, RANK)
    coarse = basis.astype(jnp.bfloat16)
    partial_value = lax.dot_general(
        coarse, jac, (((0,), (0,)), ((), ())), preferred_element_type=jnp.float32
    )
    projection = lax.psum_scatter(partial_value, "pix", scatter_dimension=0, tiled=True)
    basis_out = (own_basis * math.sqrt(total_rows)).reshape(1, 2 * share_pix, RANK)
    r_factor = lower_factor.T / math.sqrt(total_rows * ACT)
    return (basis_out, projection, r_factor)


def solution(mesh):
    return jax.shard_map(
        on_device,
        mesh=mesh,
        in_specs=(
            P("pix", None),
            P("act"),
            P("act", None),
            P("pix", None, "act"),
            P("pix"),
            P("pix"),
        ),
        out_specs=(P("pix", "act", None), P("pix", "act"), P()),
        check_vma=False,
    )
```

```python
import math

import jax
import jax.numpy as jnp
from jax import lax
from jax.sharding import PartitionSpec as P

GRID = 128
FOCAL = 256
RANK = 128
ACT = 32768


TWO_PI = 2.0 * math.pi
INFL_RATE = 4.5
DEFOCUS_RATE = 6.0


def rows_for(lines, count):
    spare = -len(lines) % count
    return jnp.pad(lines, [(0, spare)] + [(0, 0)] * (lines.ndim - 1))


def sent_to_all(value, axis):
    copies = jnp.broadcast_to(value, (lax.axis_size(axis), *value.shape))
    return lax.all_to_all(copies, axis, split_axis=0, concat_axis=0, tiled=True)


def laid_out(parts, dim):
    shape = list(parts.shape[1:])
    shape[dim] *= parts.shape[0]
    return jnp.moveaxis(parts, 0, dim).reshape(shape)


def collect(value, axis, dim):
    parts = sent_to_all(value, axis)
    return laid_out(parts, dim)


def in_blocks(value, dim, count):
    before, after = (value.shape[:dim], value.shape[dim + 1 :])
    return jnp.moveaxis(value.reshape(*before, count, -1, *after), dim, 0)


def summed_on_arrival(value, axis, dim):
    parts = in_blocks(value, dim, lax.axis_size(axis))
    arrived = lax.all_to_all(parts, axis, split_axis=0, concat_axis=0, tiled=True)
    return arrived.sum(axis=0)


def sum_by_parts(value, axes):
    lines = value.reshape(-1, value.shape[-1])
    padded = rows_for(lines, lax.axis_size(axes))
    whole = collect(summed_on_arrival(padded, axes, 0), axes, 0)
    return lax.slice_in_dim(whole, 0, len(lines)).reshape(value.shape)


def butterfly_sum(value, axis):
    count = lax.axis_size(axis)
    step = 1
    while step < count:
        pairs = [(i, i ^ step) for i in range(count)]
        value = value + lax.ppermute(value, axis, pairs)
        step *= 2
    return value


def jacobian_planes(pixels, wave_scale, flux_level, codes, field_re, field_im):
    delta_u = pixels // FOCAL - FOCAL // 2
    delta_v = pixels % FOCAL - FOCAL // 2
    mirror = codes // (GRID * GRID)
    column_x = codes // GRID % GRID - GRID // 2
    column_y = codes % GRID - GRID // 2
    phase_int = delta_u[:, None] * column_x[None, :] + delta_v[:, None] * column_y[None, :]
    radius = (delta_u * delta_u + delta_v * delta_v).astype(jnp.float32)
    amplitude = flux_level * jnp.exp(-INFL_RATE * radius / (FOCAL * FOCAL))
    defocus = radius * (TWO_PI * DEFOCUS_RATE / (FOCAL * FOCAL)) / wave_scale
    phase_angle = mirror.astype(jnp.float32)[None, :] * defocus[
        :, None
    ] - TWO_PI / FOCAL * wave_scale * phase_int.astype(jnp.float32)
    cosine = jnp.cos(phase_angle)
    sine_part = jnp.sin(phase_angle)
    real_part = amplitude[:, None] * (field_re[None, :] * cosine - field_im[None, :] * sine_part)
    imag_part = amplitude[:, None] * (field_re[None, :] * sine_part + field_im[None, :] * cosine)
    return real_part.astype(jnp.bfloat16), imag_part.astype(jnp.bfloat16)


def gram_of(sketch):
    return lax.dot_general(
        sketch,
        sketch,
        (((0,), (0,)), ((), ())),
        precision=lax.Precision.HIGHEST,
        preferred_element_type=jnp.float32,
    )


def on_device(pixel_index, act_map, omega, pupil_field, channel_scale, channel_flux):
    pixels = pixel_index[0]
    npix = pixels.shape[0]
    rows_dev = 2 * npix
    act_count = lax.axis_size("act")
    pix_count = lax.axis_size("pix")
    total_rows = rows_dev * pix_count
    share_pix = npix // act_count
    real_rows, imag_rows = jacobian_planes(
        pixels, channel_scale[0], channel_flux[0], act_map, pupil_field[0, 0], pupil_field[0, 1]
    )
    jac = jnp.concatenate([real_rows, imag_rows], axis=0)
    partial_sketch = jnp.dot(jac, omega, preferred_element_type=jnp.float32)
    sketch = sum_by_parts(partial_sketch, "act")
    gram_matrix = butterfly_sum(gram_of(sketch), "pix")
    lower_factor = jnp.linalg.cholesky(gram_matrix)
    basis = jax.scipy.linalg.solve_triangular(lower_factor, sketch.T, lower=True).T
    first = lax.axis_index("act") * share_pix
    own_re = lax.dynamic_slice_in_dim(basis, first, share_pix, 0)
    own_im = lax.dynamic_slice_in_dim(basis, npix + first, share_pix, 0)
    own_basis = jnp.stack([own_re, own_im], axis=1).reshape(2 * share_pix, RANK)
    coarse = basis.astype(jnp.bfloat16)
    partial_value = lax.dot_general(
        coarse, jac, (((0,), (0,)), ((), ())), preferred_element_type=jnp.float32
    )
    projection = summed_on_arrival(partial_value, "pix", 0)
    basis_out = (own_basis * math.sqrt(total_rows)).reshape(1, 2 * share_pix, RANK)
    r_factor = lower_factor.T / math.sqrt(total_rows * ACT)
    return (basis_out, projection, r_factor)


def solution(mesh):
    return jax.shard_map(
        on_device,
        mesh=mesh,
        in_specs=(
            P("pix", None),
            P("act"),
            P("act", None),
            P("pix", None, "act"),
            P("pix"),
            P("pix"),
        ),
        out_specs=(P("pix", "act", None), P("pix", "act"), P()),
        check_vma=False,
    )
```

```python
import math

import jax
import jax.numpy as jnp
from jax import lax
from jax.experimental import pallas as pl
from jax.experimental.pallas import tpu as pltpu
from jax.sharding import PartitionSpec as P

GRID = 128
FOCAL = 256
RANK = 128
ACT = 32768


TWO_PI = 2.0 * math.pi
INFL_RATE = 4.5
DEFOCUS_RATE = 6.0


def rows_for(lines, count):
    spare = -len(lines) % count
    return jnp.pad(lines, [(0, spare)] + [(0, 0)] * (lines.ndim - 1))


def sent_to_all(value, axis):
    copies = jnp.broadcast_to(value, (lax.axis_size(axis), *value.shape))
    return lax.all_to_all(copies, axis, split_axis=0, concat_axis=0, tiled=True)


def laid_out(parts, dim):
    shape = list(parts.shape[1:])
    shape[dim] *= parts.shape[0]
    return jnp.moveaxis(parts, 0, dim).reshape(shape)


def collect(value, axis, dim):
    parts = sent_to_all(value, axis)
    return laid_out(parts, dim)


def in_blocks(value, dim, count):
    before, after = (value.shape[:dim], value.shape[dim + 1 :])
    return jnp.moveaxis(value.reshape(*before, count, -1, *after), dim, 0)


def summed_on_arrival(value, axis, dim):
    parts = in_blocks(value, dim, lax.axis_size(axis))
    arrived = lax.all_to_all(parts, axis, split_axis=0, concat_axis=0, tiled=True)
    return arrived.sum(axis=0)


def sum_by_parts(value, axes):
    lines = value.reshape(-1, value.shape[-1])
    padded = rows_for(lines, lax.axis_size(axes))
    whole = collect(summed_on_arrival(padded, axes, 0), axes, 0)
    return lax.slice_in_dim(whole, 0, len(lines)).reshape(value.shape)


def butterfly_sum(value, axis):
    count = lax.axis_size(axis)
    step = 1
    while step < count:
        pairs = [(i, i ^ step) for i in range(count)]
        value = value + lax.ppermute(value, axis, pairs)
        step *= 2
    return value


def chol_inv_kernel(g_ref, lt_ref, inv_ref):
    n = g_ref.shape[0]
    lt_ref[...] = g_ref[...]
    rows = lax.broadcasted_iota(jnp.int32, (n, n), 0)
    cols = lax.broadcasted_iota(jnp.int32, (n, n), 1)
    inv_ref[...] = jnp.where(rows == cols, 1.0, 0.0).astype(jnp.float32)
    lane = lax.broadcasted_iota(jnp.int32, (1, n), 1)
    sub = lax.broadcasted_iota(jnp.int32, (n, 1), 0)

    def step(j, carry):
        a = lt_ref[...]
        row = lt_ref[pl.ds(j, 1), :]
        d = jnp.sum(jnp.where(lane == j, row, 0.0), axis=1, keepdims=True)
        r = lax.rsqrt(d)
        l = jnp.where(lane >= j, row * r, 0.0)
        colj = jnp.sum(jnp.where(cols == j, a, 0.0), axis=1, keepdims=True)
        c = jnp.where(sub > j, colj * r, 0.0)
        b_row = inv_ref[pl.ds(j, 1), :] * r
        lt_ref[...] = a - c * l
        inv_ref[...] = inv_ref[...] - c * b_row
        lt_ref[pl.ds(j, 1), :] = l
        inv_ref[pl.ds(j, 1), :] = b_row
        return carry

    lax.fori_loop(0, n, step, 0)


def chol_inv(g):
    n = g.shape[0]
    return pl.pallas_call(
        chol_inv_kernel,
        out_shape=(
            jax.ShapeDtypeStruct((n, n), jnp.float32),
            jax.ShapeDtypeStruct((n, n), jnp.float32),
        ),
        in_specs=[pl.BlockSpec(memory_space=pltpu.VMEM)],
        out_specs=(pl.BlockSpec(memory_space=pltpu.VMEM), pl.BlockSpec(memory_space=pltpu.VMEM)),
    )(g)


def jacobian_planes(pixels, wave_scale, flux_level, codes, field_re, field_im):
    delta_u = pixels // FOCAL - FOCAL // 2
    delta_v = pixels % FOCAL - FOCAL // 2
    mirror = codes // (GRID * GRID)
    column_x = codes // GRID % GRID - GRID // 2
    column_y = codes % GRID - GRID // 2
    phase_int = delta_u[:, None] * column_x[None, :] + delta_v[:, None] * column_y[None, :]
    radius = (delta_u * delta_u + delta_v * delta_v).astype(jnp.float32)
    amplitude = flux_level * jnp.exp(-INFL_RATE * radius / (FOCAL * FOCAL))
    defocus = radius * (TWO_PI * DEFOCUS_RATE / (FOCAL * FOCAL)) / wave_scale
    phase_angle = mirror.astype(jnp.float32)[None, :] * defocus[
        :, None
    ] - TWO_PI / FOCAL * wave_scale * phase_int.astype(jnp.float32)
    cosine = jnp.cos(phase_angle)
    sine_part = jnp.sin(phase_angle)
    real_part = amplitude[:, None] * (field_re[None, :] * cosine - field_im[None, :] * sine_part)
    imag_part = amplitude[:, None] * (field_re[None, :] * sine_part + field_im[None, :] * cosine)
    return real_part.astype(jnp.bfloat16), imag_part.astype(jnp.bfloat16)


def gram_of(sketch):
    return lax.dot_general(
        sketch,
        sketch,
        (((0,), (0,)), ((), ())),
        precision=lax.Precision.HIGHEST,
        preferred_element_type=jnp.float32,
    )


def on_device(pixel_index, act_map, omega, pupil_field, channel_scale, channel_flux):
    pixels = pixel_index[0]
    npix = pixels.shape[0]
    rows_dev = 2 * npix
    act_count = lax.axis_size("act")
    pix_count = lax.axis_size("pix")
    total_rows = rows_dev * pix_count
    share_pix = npix // act_count
    real_rows, imag_rows = jacobian_planes(
        pixels, channel_scale[0], channel_flux[0], act_map, pupil_field[0, 0], pupil_field[0, 1]
    )
    jac = jnp.concatenate([real_rows, imag_rows], axis=0)
    partial_sketch = jnp.dot(jac, omega, preferred_element_type=jnp.float32)
    sketch = sum_by_parts(partial_sketch, "act")
    gram_matrix = butterfly_sum(gram_of(sketch), "pix")
    upper_factor, lower_inverse = chol_inv(gram_matrix)
    basis = lax.dot_general(
        sketch,
        lower_inverse,
        (((1,), (1,)), ((), ())),
        precision=lax.Precision.HIGHEST,
        preferred_element_type=jnp.float32,
    )
    first = lax.axis_index("act") * share_pix
    own_re = lax.dynamic_slice_in_dim(basis, first, share_pix, 0)
    own_im = lax.dynamic_slice_in_dim(basis, npix + first, share_pix, 0)
    own_basis = jnp.stack([own_re, own_im], axis=1).reshape(2 * share_pix, RANK)
    coarse = basis.astype(jnp.bfloat16)
    partial_value = lax.dot_general(
        coarse, jac, (((0,), (0,)), ((), ())), preferred_element_type=jnp.float32
    )
    projection = summed_on_arrival(partial_value, "pix", 0)
    basis_out = (own_basis * math.sqrt(total_rows)).reshape(1, 2 * share_pix, RANK)
    r_factor = upper_factor / math.sqrt(total_rows * ACT)
    return (basis_out, projection, r_factor)


def solution(mesh):
    return jax.shard_map(
        on_device,
        mesh=mesh,
        in_specs=(
            P("pix", None),
            P("act"),
            P("act", None),
            P("pix", None, "act"),
            P("pix"),
            P("pix"),
        ),
        out_specs=(P("pix", "act", None), P("pix", "act"), P()),
        check_vma=False,
    )
```

```python
import math

import jax
import jax.numpy as jnp
from jax import lax
from jax.experimental import pallas as pl
from jax.experimental.pallas import tpu as pltpu
from jax.sharding import PartitionSpec as P

GRID = 128
FOCAL = 256
RANK = 128
ACT = 32768


TWO_PI = 2.0 * math.pi
INFL_RATE = 4.5
DEFOCUS_RATE = 6.0


def rows_for(lines, count):
    spare = -len(lines) % count
    return jnp.pad(lines, [(0, spare)] + [(0, 0)] * (lines.ndim - 1))


def sent_to_all(value, axis):
    copies = jnp.broadcast_to(value, (lax.axis_size(axis), *value.shape))
    return lax.all_to_all(copies, axis, split_axis=0, concat_axis=0, tiled=True)


def laid_out(parts, dim):
    shape = list(parts.shape[1:])
    shape[dim] *= parts.shape[0]
    return jnp.moveaxis(parts, 0, dim).reshape(shape)


def collect(value, axis, dim):
    parts = sent_to_all(value, axis)
    return laid_out(parts, dim)


def in_blocks(value, dim, count):
    before, after = (value.shape[:dim], value.shape[dim + 1 :])
    return jnp.moveaxis(value.reshape(*before, count, -1, *after), dim, 0)


def summed_on_arrival(value, axis, dim):
    parts = in_blocks(value, dim, lax.axis_size(axis))
    arrived = lax.all_to_all(parts, axis, split_axis=0, concat_axis=0, tiled=True)
    return arrived.sum(axis=0)


def sum_by_parts(value, axes):
    lines = value.reshape(-1, value.shape[-1])
    padded = rows_for(lines, lax.axis_size(axes))
    whole = collect(summed_on_arrival(padded, axes, 0), axes, 0)
    return lax.slice_in_dim(whole, 0, len(lines)).reshape(value.shape)


def butterfly_sum(value, axis):
    count = lax.axis_size(axis)
    step = 1
    while step < count:
        pairs = [(i, i ^ step) for i in range(count)]
        value = value + lax.ppermute(value, axis, pairs)
        step *= 2
    return value


def chol_inv_kernel(g_ref, lt_ref, inv_ref):
    n = g_ref.shape[0]
    lt_ref[...] = g_ref[...]
    rows = lax.broadcasted_iota(jnp.int32, (n, n), 0)
    cols = lax.broadcasted_iota(jnp.int32, (n, n), 1)
    inv_ref[...] = jnp.where(rows == cols, 1.0, 0.0).astype(jnp.float32)
    lane = lax.broadcasted_iota(jnp.int32, (1, n), 1)
    sub = lax.broadcasted_iota(jnp.int32, (n, 1), 0)
    for j in range(n):
        row = lt_ref[j : j + 1, :]
        d = jnp.sum(jnp.where(lane == j, row, 0.0), axis=1, keepdims=True)
        r = lax.rsqrt(d)
        l = jnp.where(lane >= j, row * r, 0.0)
        b_row = inv_ref[j : j + 1, :] * r
        if j + 1 < n:
            t = (j + 1) // 8 * 8
            col = jnp.broadcast_to(l, (8, n)).T[:, 0:1]
            c = jnp.where(sub > j, col, 0.0)[t:]
            lt_ref[t:, :] = lt_ref[t:, :] - c * l
            inv_ref[t:, :] = inv_ref[t:, :] - c * b_row
        lt_ref[j : j + 1, :] = l
        inv_ref[j : j + 1, :] = b_row


def chol_inv(g):
    n = g.shape[0]
    return pl.pallas_call(
        chol_inv_kernel,
        out_shape=(
            jax.ShapeDtypeStruct((n, n), jnp.float32),
            jax.ShapeDtypeStruct((n, n), jnp.float32),
        ),
        in_specs=[pl.BlockSpec(memory_space=pltpu.VMEM)],
        out_specs=(pl.BlockSpec(memory_space=pltpu.VMEM), pl.BlockSpec(memory_space=pltpu.VMEM)),
    )(g)


def jacobian_planes(pixels, wave_scale, flux_level, codes, field_re, field_im):
    delta_u = pixels // FOCAL - FOCAL // 2
    delta_v = pixels % FOCAL - FOCAL // 2
    mirror = codes // (GRID * GRID)
    column_x = codes // GRID % GRID - GRID // 2
    column_y = codes % GRID - GRID // 2
    phase_int = delta_u[:, None] * column_x[None, :] + delta_v[:, None] * column_y[None, :]
    radius = (delta_u * delta_u + delta_v * delta_v).astype(jnp.float32)
    amplitude = flux_level * jnp.exp(-INFL_RATE * radius / (FOCAL * FOCAL))
    defocus = radius * (TWO_PI * DEFOCUS_RATE / (FOCAL * FOCAL)) / wave_scale
    phase_angle = mirror.astype(jnp.float32)[None, :] * defocus[
        :, None
    ] - TWO_PI / FOCAL * wave_scale * phase_int.astype(jnp.float32)
    cosine = jnp.cos(phase_angle)
    sine_part = jnp.sin(phase_angle)
    real_part = amplitude[:, None] * (field_re[None, :] * cosine - field_im[None, :] * sine_part)
    imag_part = amplitude[:, None] * (field_re[None, :] * sine_part + field_im[None, :] * cosine)
    return real_part.astype(jnp.bfloat16), imag_part.astype(jnp.bfloat16)


def gram_of(sketch):
    return lax.dot_general(
        sketch,
        sketch,
        (((0,), (0,)), ((), ())),
        precision=lax.Precision.HIGHEST,
        preferred_element_type=jnp.float32,
    )


def on_device(pixel_index, act_map, omega, pupil_field, channel_scale, channel_flux):
    pixels = pixel_index[0]
    npix = pixels.shape[0]
    rows_dev = 2 * npix
    act_count = lax.axis_size("act")
    pix_count = lax.axis_size("pix")
    total_rows = rows_dev * pix_count
    share_pix = npix // act_count
    real_rows, imag_rows = jacobian_planes(
        pixels, channel_scale[0], channel_flux[0], act_map, pupil_field[0, 0], pupil_field[0, 1]
    )
    jac = jnp.concatenate([real_rows, imag_rows], axis=0)
    partial_sketch = jnp.dot(jac, omega, preferred_element_type=jnp.float32)
    sketch = sum_by_parts(partial_sketch, "act")
    gram_matrix = butterfly_sum(gram_of(sketch), "pix")
    upper_factor, lower_inverse = chol_inv(gram_matrix)
    basis = lax.dot_general(
        sketch,
        lower_inverse,
        (((1,), (1,)), ((), ())),
        precision=lax.Precision.HIGHEST,
        preferred_element_type=jnp.float32,
    )
    first = lax.axis_index("act") * share_pix
    own_re = lax.dynamic_slice_in_dim(basis, first, share_pix, 0)
    own_im = lax.dynamic_slice_in_dim(basis, npix + first, share_pix, 0)
    own_basis = jnp.stack([own_re, own_im], axis=1).reshape(2 * share_pix, RANK)
    coarse = basis.astype(jnp.bfloat16)
    partial_value = lax.dot_general(
        coarse, jac, (((0,), (0,)), ((), ())), preferred_element_type=jnp.float32
    )
    projection = summed_on_arrival(partial_value, "pix", 0)
    basis_out = (own_basis * math.sqrt(total_rows)).reshape(1, 2 * share_pix, RANK)
    r_factor = upper_factor / math.sqrt(total_rows * ACT)
    return (basis_out, projection, r_factor)


def solution(mesh):
    return jax.shard_map(
        on_device,
        mesh=mesh,
        in_specs=(
            P("pix", None),
            P("act"),
            P("act", None),
            P("pix", None, "act"),
            P("pix"),
            P("pix"),
        ),
        out_specs=(P("pix", "act", None), P("pix", "act"), P()),
        check_vma=False,
    )
```

```python
import math

import jax
import jax.numpy as jnp
from jax import lax
from jax.experimental import pallas as pl
from jax.experimental.pallas import tpu as pltpu
from jax.sharding import PartitionSpec as P

GRID = 128
FOCAL = 256
RANK = 128
ACT = 32768


TWO_PI = 2.0 * math.pi
INFL_RATE = 4.5
DEFOCUS_RATE = 6.0


def rows_for(lines, count):
    spare = -len(lines) % count
    return jnp.pad(lines, [(0, spare)] + [(0, 0)] * (lines.ndim - 1))


def sent_to_all(value, axis):
    copies = jnp.broadcast_to(value, (lax.axis_size(axis), *value.shape))
    return lax.all_to_all(copies, axis, split_axis=0, concat_axis=0, tiled=True)


def laid_out(parts, dim):
    shape = list(parts.shape[1:])
    shape[dim] *= parts.shape[0]
    return jnp.moveaxis(parts, 0, dim).reshape(shape)


def collect(value, axis, dim):
    parts = sent_to_all(value, axis)
    return laid_out(parts, dim)


def in_blocks(value, dim, count):
    before, after = (value.shape[:dim], value.shape[dim + 1 :])
    return jnp.moveaxis(value.reshape(*before, count, -1, *after), dim, 0)


def summed_on_arrival(value, axis, dim):
    parts = in_blocks(value, dim, lax.axis_size(axis))
    arrived = lax.all_to_all(parts, axis, split_axis=0, concat_axis=0, tiled=True)
    return arrived.sum(axis=0)


def sum_by_parts(value, axes):
    lines = value.reshape(-1, value.shape[-1])
    padded = rows_for(lines, lax.axis_size(axes))
    whole = collect(summed_on_arrival(padded, axes, 0), axes, 0)
    return lax.slice_in_dim(whole, 0, len(lines)).reshape(value.shape)


def butterfly_sum(value, axis):
    count = lax.axis_size(axis)
    step = 1
    while step < count:
        pairs = [(i, i ^ step) for i in range(count)]
        value = value + lax.ppermute(value, axis, pairs)
        step *= 2
    return value


def chol_inv_kernel(g_ref, lt_ref, inv_ref):
    n = g_ref.shape[0]
    lt_ref[...] = g_ref[...]
    rows = lax.broadcasted_iota(jnp.int32, (n, n), 0)
    cols = lax.broadcasted_iota(jnp.int32, (n, n), 1)
    inv_ref[...] = jnp.where(rows == cols, 1.0, 0.0).astype(jnp.float32)
    lane = lax.broadcasted_iota(jnp.int32, (1, n), 1)
    sub = lax.broadcasted_iota(jnp.int32, (n, 1), 0)

    def step(j, carry):
        a = lt_ref[...]
        row = lt_ref[pl.ds(j, 1), :]
        d = jnp.sum(jnp.where(lane == j, row, 0.0), axis=1, keepdims=True)
        r = lax.rsqrt(d)
        l = jnp.where(lane >= j, row * r, 0.0)
        colj = jnp.sum(jnp.where(cols == j, a, 0.0), axis=1, keepdims=True)
        c = jnp.where(sub > j, colj * r, 0.0)
        b_row = inv_ref[pl.ds(j, 1), :] * r
        lt_ref[...] = a - c * l
        inv_ref[...] = inv_ref[...] - c * b_row
        lt_ref[pl.ds(j, 1), :] = l
        inv_ref[pl.ds(j, 1), :] = b_row
        return carry

    lax.fori_loop(0, n, step, 0)


def chol_inv(g):
    n = g.shape[0]
    return pl.pallas_call(
        chol_inv_kernel,
        out_shape=(
            jax.ShapeDtypeStruct((n, n), jnp.float32),
            jax.ShapeDtypeStruct((n, n), jnp.float32),
        ),
        in_specs=[pl.BlockSpec(memory_space=pltpu.VMEM)],
        out_specs=(pl.BlockSpec(memory_space=pltpu.VMEM), pl.BlockSpec(memory_space=pltpu.VMEM)),
    )(g)


def jacobian_planes(pixels, wave_scale, flux_level, codes, field_re, field_im):
    delta_u = pixels // FOCAL - FOCAL // 2
    delta_v = pixels % FOCAL - FOCAL // 2
    mirror = codes // (GRID * GRID)
    column_x = codes // GRID % GRID - GRID // 2
    column_y = codes % GRID - GRID // 2
    phase_int = delta_u[:, None] * column_x[None, :] + delta_v[:, None] * column_y[None, :]
    radius = (delta_u * delta_u + delta_v * delta_v).astype(jnp.float32)
    amplitude = flux_level * jnp.exp(-INFL_RATE * radius / (FOCAL * FOCAL))
    defocus = radius * (TWO_PI * DEFOCUS_RATE / (FOCAL * FOCAL)) / wave_scale
    phase_angle = mirror.astype(jnp.float32)[None, :] * defocus[
        :, None
    ] - TWO_PI / FOCAL * wave_scale * phase_int.astype(jnp.float32)
    cosine = jnp.cos(phase_angle)
    sine_part = jnp.sin(phase_angle)
    real_part = amplitude[:, None] * (field_re[None, :] * cosine - field_im[None, :] * sine_part)
    imag_part = amplitude[:, None] * (field_re[None, :] * sine_part + field_im[None, :] * cosine)
    return real_part.astype(jnp.bfloat16), imag_part.astype(jnp.bfloat16)


def gram_of(sketch):
    return lax.dot_general(
        sketch,
        sketch,
        (((0,), (0,)), ((), ())),
        precision=lax.Precision.HIGHEST,
        preferred_element_type=jnp.float32,
    )


def on_device(pixel_index, act_map, omega, pupil_field, channel_scale, channel_flux):
    pixels = pixel_index[0]
    npix = pixels.shape[0]
    rows_dev = 2 * npix
    act_count = lax.axis_size("act")
    pix_count = lax.axis_size("pix")
    total_rows = rows_dev * pix_count
    share_pix = npix // act_count
    real_rows, imag_rows = jacobian_planes(
        pixels, channel_scale[0], channel_flux[0], act_map, pupil_field[0, 0], pupil_field[0, 1]
    )
    jac = jnp.concatenate([real_rows, imag_rows], axis=0)
    partial_sketch = jnp.dot(jac, omega, preferred_element_type=jnp.float32)
    sketch = sum_by_parts(partial_sketch, "act")
    through = lax.dot_general(
        sketch,
        jac,
        (((0,), (0,)), ((), ())),
        precision=lax.Precision.HIGH,
        preferred_element_type=jnp.float32,
    )
    summed = butterfly_sum(jnp.concatenate([gram_of(sketch), through], axis=1), "pix")
    gram_matrix = summed[:, :RANK]
    through_sum = summed[:, RANK:]
    upper_factor, lower_inverse = chol_inv(gram_matrix)
    first = lax.axis_index("act") * share_pix
    own_re = lax.dynamic_slice_in_dim(sketch, first, share_pix, 0)
    own_im = lax.dynamic_slice_in_dim(sketch, npix + first, share_pix, 0)
    own_sketch = jnp.stack([own_re, own_im], axis=1).reshape(2 * share_pix, RANK)
    own_basis = lax.dot_general(
        own_sketch,
        lower_inverse,
        (((1,), (1,)), ((), ())),
        precision=lax.Precision.HIGHEST,
        preferred_element_type=jnp.float32,
    )
    rank_rows = RANK // pix_count
    own_inverse = lax.dynamic_slice_in_dim(lower_inverse, lax.axis_index("pix") * rank_rows, rank_rows, 0)
    projection = jnp.dot(
        own_inverse, through_sum, precision=lax.Precision.HIGHEST, preferred_element_type=jnp.float32
    )
    basis_out = (own_basis * math.sqrt(total_rows)).reshape(1, 2 * share_pix, RANK)
    r_factor = upper_factor / math.sqrt(total_rows * ACT)
    return (basis_out, projection, r_factor)


def solution(mesh):
    return jax.shard_map(
        on_device,
        mesh=mesh,
        in_specs=(
            P("pix", None),
            P("act"),
            P("act", None),
            P("pix", None, "act"),
            P("pix"),
            P("pix"),
        ),
        out_specs=(P("pix", "act", None), P("pix", "act"), P()),
        check_vma=False,
    )
```

```python
import math

import jax
import jax.numpy as jnp
from jax import lax
from jax.experimental import pallas as pl
from jax.experimental.pallas import tpu as pltpu
from jax.sharding import PartitionSpec as P

GRID = 128
FOCAL = 256
RANK = 128
ACT = 32768


TWO_PI = 2.0 * math.pi
INFL_RATE = 4.5
DEFOCUS_RATE = 6.0


def rows_for(lines, count):
    spare = -len(lines) % count
    return jnp.pad(lines, [(0, spare)] + [(0, 0)] * (lines.ndim - 1))


def sent_to_all(value, axis):
    copies = jnp.broadcast_to(value, (lax.axis_size(axis), *value.shape))
    return lax.all_to_all(copies, axis, split_axis=0, concat_axis=0, tiled=True)


def laid_out(parts, dim):
    shape = list(parts.shape[1:])
    shape[dim] *= parts.shape[0]
    return jnp.moveaxis(parts, 0, dim).reshape(shape)


def collect(value, axis, dim):
    parts = sent_to_all(value, axis)
    return laid_out(parts, dim)


def in_blocks(value, dim, count):
    before, after = (value.shape[:dim], value.shape[dim + 1 :])
    return jnp.moveaxis(value.reshape(*before, count, -1, *after), dim, 0)


def summed_on_arrival(value, axis, dim):
    parts = in_blocks(value, dim, lax.axis_size(axis))
    arrived = lax.all_to_all(parts, axis, split_axis=0, concat_axis=0, tiled=True)
    return arrived.sum(axis=0)


def sum_by_parts(value, axes):
    lines = value.reshape(-1, value.shape[-1])
    padded = rows_for(lines, lax.axis_size(axes))
    whole = collect(summed_on_arrival(padded, axes, 0), axes, 0)
    return lax.slice_in_dim(whole, 0, len(lines)).reshape(value.shape)


def butterfly_sum(value, axis):
    count = lax.axis_size(axis)
    step = 1
    while step < count:
        pairs = [(i, i ^ step) for i in range(count)]
        value = value + lax.ppermute(value, axis, pairs)
        step *= 2
    return value


def chol_inv_kernel(g_ref, lt_ref, inv_ref):
    n = g_ref.shape[0]
    lt_ref[...] = g_ref[...]
    rows = lax.broadcasted_iota(jnp.int32, (n, n), 0)
    cols = lax.broadcasted_iota(jnp.int32, (n, n), 1)
    inv_ref[...] = jnp.where(rows == cols, 1.0, 0.0).astype(jnp.float32)
    lane = lax.broadcasted_iota(jnp.int32, (1, n), 1)
    sub = lax.broadcasted_iota(jnp.int32, (n, 1), 0)

    def step(j, carry):
        a = lt_ref[...]
        row = lt_ref[pl.ds(j, 1), :]
        d = jnp.sum(jnp.where(lane == j, row, 0.0), axis=1, keepdims=True)
        r = lax.rsqrt(d)
        l = jnp.where(lane >= j, row * r, 0.0)
        colj = jnp.sum(jnp.where(cols == j, a, 0.0), axis=1, keepdims=True)
        c = jnp.where(sub > j, colj * r, 0.0)
        b_row = inv_ref[pl.ds(j, 1), :] * r
        lt_ref[...] = a - c * l
        inv_ref[...] = inv_ref[...] - c * b_row
        lt_ref[pl.ds(j, 1), :] = l
        inv_ref[pl.ds(j, 1), :] = b_row
        return carry

    lax.fori_loop(0, n, step, 0)


def chol_inv(g):
    n = g.shape[0]
    return pl.pallas_call(
        chol_inv_kernel,
        out_shape=(
            jax.ShapeDtypeStruct((n, n), jnp.float32),
            jax.ShapeDtypeStruct((n, n), jnp.float32),
        ),
        in_specs=[pl.BlockSpec(memory_space=pltpu.VMEM)],
        out_specs=(pl.BlockSpec(memory_space=pltpu.VMEM), pl.BlockSpec(memory_space=pltpu.VMEM)),
    )(g)


def jacobian_planes(pixels, wave_scale, flux_level, codes, field_re, field_im):
    delta_u = pixels // FOCAL - FOCAL // 2
    delta_v = pixels % FOCAL - FOCAL // 2
    mirror = codes // (GRID * GRID)
    column_x = codes // GRID % GRID - GRID // 2
    column_y = codes % GRID - GRID // 2
    phase_int = delta_u[:, None] * column_x[None, :] + delta_v[:, None] * column_y[None, :]
    radius = (delta_u * delta_u + delta_v * delta_v).astype(jnp.float32)
    amplitude = flux_level * jnp.exp(-INFL_RATE * radius / (FOCAL * FOCAL))
    defocus = radius * (TWO_PI * DEFOCUS_RATE / (FOCAL * FOCAL)) / wave_scale
    phase_angle = mirror.astype(jnp.float32)[None, :] * defocus[
        :, None
    ] - TWO_PI / FOCAL * wave_scale * phase_int.astype(jnp.float32)
    cosine = jnp.cos(phase_angle)
    sine_part = jnp.sin(phase_angle)
    real_part = amplitude[:, None] * (field_re[None, :] * cosine - field_im[None, :] * sine_part)
    imag_part = amplitude[:, None] * (field_re[None, :] * sine_part + field_im[None, :] * cosine)
    return real_part.astype(jnp.bfloat16), imag_part.astype(jnp.bfloat16)


def gram_of(sketch):
    return lax.dot_general(
        sketch,
        sketch,
        (((0,), (0,)), ((), ())),
        precision=lax.Precision.HIGHEST,
        preferred_element_type=jnp.float32,
    )


def on_device(pixel_index, act_map, omega, pupil_field, channel_scale, channel_flux):
    pixels = pixel_index[0]
    npix = pixels.shape[0]
    rows_dev = 2 * npix
    act_count = lax.axis_size("act")
    pix_count = lax.axis_size("pix")
    total_rows = rows_dev * pix_count
    share_pix = npix // act_count
    real_rows, imag_rows = jacobian_planes(
        pixels, channel_scale[0], channel_flux[0], act_map, pupil_field[0, 0], pupil_field[0, 1]
    )
    jac = jnp.concatenate([real_rows, imag_rows], axis=0)
    partial_sketch = jnp.dot(jac, omega, preferred_element_type=jnp.float32)
    sketch = sum_by_parts(partial_sketch, "act")
    gram_matrix = butterfly_sum(gram_of(sketch), "pix")
    upper_factor, lower_inverse = chol_inv(gram_matrix)
    basis = lax.dot_general(
        sketch,
        lower_inverse,
        (((1,), (1,)), ((), ())),
        precision=lax.Precision.HIGHEST,
        preferred_element_type=jnp.float32,
    )
    first = lax.axis_index("act") * share_pix
    own_re = lax.dynamic_slice_in_dim(basis, first, share_pix, 0)
    own_im = lax.dynamic_slice_in_dim(basis, npix + first, share_pix, 0)
    own_basis = jnp.stack([own_re, own_im], axis=1).reshape(2 * share_pix, RANK)
    coarse = basis.astype(jnp.bfloat16)
    partial_value = lax.dot_general(
        coarse, jac, (((0,), (0,)), ((), ())), preferred_element_type=jnp.float32
    )
    parts = in_blocks(partial_value.astype(jnp.bfloat16), 0, pix_count)
    arrived = lax.all_to_all(parts, "pix", split_axis=0, concat_axis=0, tiled=True)
    projection = arrived.astype(jnp.float32).sum(axis=0)
    basis_out = (own_basis * math.sqrt(total_rows)).reshape(1, 2 * share_pix, RANK)
    r_factor = upper_factor / math.sqrt(total_rows * ACT)
    return (basis_out, projection, r_factor)


def solution(mesh):
    return jax.shard_map(
        on_device,
        mesh=mesh,
        in_specs=(
            P("pix", None),
            P("act"),
            P("act", None),
            P("pix", None, "act"),
            P("pix"),
            P("pix"),
        ),
        out_specs=(P("pix", "act", None), P("pix", "act"), P()),
        check_vma=False,
    )
```

```python
import math

import jax
import jax.numpy as jnp
from jax import lax
from jax.experimental import pallas as pl
from jax.experimental.pallas import tpu as pltpu
from jax.sharding import PartitionSpec as P

GRID = 128
FOCAL = 256
RANK = 128
ACT = 32768


TWO_PI = 2.0 * math.pi
INFL_RATE = 4.5
DEFOCUS_RATE = 6.0


def rows_for(lines, count):
    spare = -len(lines) % count
    return jnp.pad(lines, [(0, spare)] + [(0, 0)] * (lines.ndim - 1))


def sent_to_all(value, axis):
    copies = jnp.broadcast_to(value, (lax.axis_size(axis), *value.shape))
    return lax.all_to_all(copies, axis, split_axis=0, concat_axis=0, tiled=True)


def laid_out(parts, dim):
    shape = list(parts.shape[1:])
    shape[dim] *= parts.shape[0]
    return jnp.moveaxis(parts, 0, dim).reshape(shape)


def collect(value, axis, dim):
    parts = sent_to_all(value, axis)
    return laid_out(parts, dim)


def in_blocks(value, dim, count):
    before, after = (value.shape[:dim], value.shape[dim + 1 :])
    return jnp.moveaxis(value.reshape(*before, count, -1, *after), dim, 0)


def summed_on_arrival(value, axis, dim):
    parts = in_blocks(value, dim, lax.axis_size(axis))
    arrived = lax.all_to_all(parts, axis, split_axis=0, concat_axis=0, tiled=True)
    return arrived.sum(axis=0)


def sum_by_parts(value, axes):
    lines = value.reshape(-1, value.shape[-1])
    padded = rows_for(lines, lax.axis_size(axes))
    whole = collect(summed_on_arrival(padded, axes, 0), axes, 0)
    return lax.slice_in_dim(whole, 0, len(lines)).reshape(value.shape)


def butterfly_sum(value, axis):
    count = lax.axis_size(axis)
    step = 1
    while step < count:
        pairs = [(i, i ^ step) for i in range(count)]
        value = value + lax.ppermute(value, axis, pairs)
        step *= 2
    return value


PANEL = 8


def chol_inv_kernel(g_ref, lt_ref, inv_ref):
    n = g_ref.shape[0]
    lt_ref[...] = g_ref[...]
    rows = lax.broadcasted_iota(jnp.int32, (n, n), 0)
    cols = lax.broadcasted_iota(jnp.int32, (n, n), 1)
    inv_ref[...] = jnp.where(rows == cols, 1.0, 0.0).astype(jnp.float32)
    lane = lax.broadcasted_iota(jnp.int32, (PANEL, n), 1)
    sub = lax.broadcasted_iota(jnp.int32, (PANEL, n), 0)
    dims = (((0,), (0,)), ((), ()))
    for p0 in range(0, n, PANEL):
        a = lt_ref[p0 : p0 + PANEL, :]
        b = inv_ref[p0 : p0 + PANEL, :]
        for i in range(PANEL):
            j = p0 + i
            row = jnp.sum(jnp.where(sub == i, a, 0.0), axis=0, keepdims=True)
            d = jnp.sum(jnp.where(lane[:1] == j, row, 0.0), axis=1, keepdims=True)
            r = lax.rsqrt(d)
            l = jnp.where(lane[:1] >= j, row * r, 0.0)
            b_row = jnp.sum(jnp.where(sub == i, b, 0.0), axis=0, keepdims=True) * r
            col = jnp.sum(jnp.where(lane == j, a, 0.0), axis=1, keepdims=True)
            c = jnp.where(sub[:, :1] > i, col * r, 0.0)
            a = jnp.where(sub == i, l, a - c * l)
            b = jnp.where(sub == i, b_row, b - c * b_row)
        lt_ref[p0 : p0 + PANEL, :] = a
        inv_ref[p0 : p0 + PANEL, :] = b
        rest = p0 + PANEL
        if rest < n:
            upd_a = lax.dot_general(
                a, a, dims, precision=lax.Precision.HIGHEST, preferred_element_type=jnp.float32
            )
            upd_b = lax.dot_general(
                a, b, dims, precision=lax.Precision.HIGHEST, preferred_element_type=jnp.float32
            )
            lt_ref[rest:, :] = lt_ref[rest:, :] - upd_a[rest:]
            inv_ref[rest:, :] = inv_ref[rest:, :] - upd_b[rest:]


def chol_inv(g):
    n = g.shape[0]
    return pl.pallas_call(
        chol_inv_kernel,
        out_shape=(
            jax.ShapeDtypeStruct((n, n), jnp.float32),
            jax.ShapeDtypeStruct((n, n), jnp.float32),
        ),
        in_specs=[pl.BlockSpec(memory_space=pltpu.VMEM)],
        out_specs=(pl.BlockSpec(memory_space=pltpu.VMEM), pl.BlockSpec(memory_space=pltpu.VMEM)),
    )(g)


def jacobian_planes(pixels, wave_scale, flux_level, codes, field_re, field_im):
    delta_u = pixels // FOCAL - FOCAL // 2
    delta_v = pixels % FOCAL - FOCAL // 2
    mirror = codes // (GRID * GRID)
    column_x = codes // GRID % GRID - GRID // 2
    column_y = codes % GRID - GRID // 2
    phase_int = delta_u[:, None] * column_x[None, :] + delta_v[:, None] * column_y[None, :]
    radius = (delta_u * delta_u + delta_v * delta_v).astype(jnp.float32)
    amplitude = flux_level * jnp.exp(-INFL_RATE * radius / (FOCAL * FOCAL))
    defocus = radius * (TWO_PI * DEFOCUS_RATE / (FOCAL * FOCAL)) / wave_scale
    phase_angle = mirror.astype(jnp.float32)[None, :] * defocus[
        :, None
    ] - TWO_PI / FOCAL * wave_scale * phase_int.astype(jnp.float32)
    cosine = jnp.cos(phase_angle)
    sine_part = jnp.sin(phase_angle)
    real_part = amplitude[:, None] * (field_re[None, :] * cosine - field_im[None, :] * sine_part)
    imag_part = amplitude[:, None] * (field_re[None, :] * sine_part + field_im[None, :] * cosine)
    return real_part.astype(jnp.bfloat16), imag_part.astype(jnp.bfloat16)


def gram_of(sketch):
    return lax.dot_general(
        sketch,
        sketch,
        (((0,), (0,)), ((), ())),
        precision=lax.Precision.HIGHEST,
        preferred_element_type=jnp.float32,
    )


def on_device(pixel_index, act_map, omega, pupil_field, channel_scale, channel_flux):
    pixels = pixel_index[0]
    npix = pixels.shape[0]
    rows_dev = 2 * npix
    act_count = lax.axis_size("act")
    pix_count = lax.axis_size("pix")
    total_rows = rows_dev * pix_count
    share_pix = npix // act_count
    real_rows, imag_rows = jacobian_planes(
        pixels, channel_scale[0], channel_flux[0], act_map, pupil_field[0, 0], pupil_field[0, 1]
    )
    jac = jnp.concatenate([real_rows, imag_rows], axis=0)
    partial_sketch = jnp.dot(jac, omega, preferred_element_type=jnp.float32)
    sketch = sum_by_parts(partial_sketch, "act")
    gram_matrix = butterfly_sum(gram_of(sketch), "pix")
    upper_factor, lower_inverse = chol_inv(gram_matrix)
    basis = lax.dot_general(
        sketch,
        lower_inverse,
        (((1,), (1,)), ((), ())),
        precision=lax.Precision.HIGHEST,
        preferred_element_type=jnp.float32,
    )
    first = lax.axis_index("act") * share_pix
    own_re = lax.dynamic_slice_in_dim(basis, first, share_pix, 0)
    own_im = lax.dynamic_slice_in_dim(basis, npix + first, share_pix, 0)
    own_basis = jnp.stack([own_re, own_im], axis=1).reshape(2 * share_pix, RANK)
    coarse = basis.astype(jnp.bfloat16)
    partial_value = lax.dot_general(
        coarse, jac, (((0,), (0,)), ((), ())), preferred_element_type=jnp.float32
    )
    parts = in_blocks(partial_value.astype(jnp.bfloat16), 0, pix_count)
    arrived = lax.all_to_all(parts, "pix", split_axis=0, concat_axis=0, tiled=True)
    projection = arrived.astype(jnp.float32).sum(axis=0)
    basis_out = (own_basis * math.sqrt(total_rows)).reshape(1, 2 * share_pix, RANK)
    r_factor = upper_factor / math.sqrt(total_rows * ACT)
    return (basis_out, projection, r_factor)


def solution(mesh):
    return jax.shard_map(
        on_device,
        mesh=mesh,
        in_specs=(
            P("pix", None),
            P("act"),
            P("act", None),
            P("pix", None, "act"),
            P("pix"),
            P("pix"),
        ),
        out_specs=(P("pix", "act", None), P("pix", "act"), P()),
        check_vma=False,
    )
```

```python
import math

import jax
import jax.numpy as jnp
from jax import lax
from jax.experimental import pallas as pl
from jax.experimental.pallas import tpu as pltpu
from jax.sharding import PartitionSpec as P

GRID = 128
FOCAL = 256
RANK = 128
ACT = 32768


TWO_PI = 2.0 * math.pi
INFL_RATE = 4.5
DEFOCUS_RATE = 6.0


def rows_for(lines, count):
    spare = -len(lines) % count
    return jnp.pad(lines, [(0, spare)] + [(0, 0)] * (lines.ndim - 1))


def sent_to_all(value, axis):
    copies = jnp.broadcast_to(value, (lax.axis_size(axis), *value.shape))
    return lax.all_to_all(copies, axis, split_axis=0, concat_axis=0, tiled=True)


def laid_out(parts, dim):
    shape = list(parts.shape[1:])
    shape[dim] *= parts.shape[0]
    return jnp.moveaxis(parts, 0, dim).reshape(shape)


def collect(value, axis, dim):
    parts = sent_to_all(value, axis)
    return laid_out(parts, dim)


def in_blocks(value, dim, count):
    before, after = (value.shape[:dim], value.shape[dim + 1 :])
    return jnp.moveaxis(value.reshape(*before, count, -1, *after), dim, 0)


def summed_on_arrival(value, axis, dim):
    parts = in_blocks(value, dim, lax.axis_size(axis))
    arrived = lax.all_to_all(parts, axis, split_axis=0, concat_axis=0, tiled=True)
    return arrived.sum(axis=0)


def sum_by_parts(value, axes):
    lines = value.reshape(-1, value.shape[-1])
    padded = rows_for(lines, lax.axis_size(axes))
    whole = collect(summed_on_arrival(padded, axes, 0), axes, 0)
    return lax.slice_in_dim(whole, 0, len(lines)).reshape(value.shape)


def butterfly_sum(value, axis):
    count = lax.axis_size(axis)
    step = 1
    while step < count:
        pairs = [(i, i ^ step) for i in range(count)]
        value = value + lax.ppermute(value, axis, pairs)
        step *= 2
    return value


def chol_inv_kernel(g_ref, lt_ref, inv_ref):
    n = g_ref.shape[0]
    lt_ref[...] = g_ref[...]
    rows = lax.broadcasted_iota(jnp.int32, (n, n), 0)
    cols = lax.broadcasted_iota(jnp.int32, (n, n), 1)
    inv_ref[...] = jnp.where(rows == cols, 1.0, 0.0).astype(jnp.float32)
    lane = lax.broadcasted_iota(jnp.int32, (1, n), 1)
    sub = lax.broadcasted_iota(jnp.int32, (n, 1), 0)

    def step(j, carry):
        a = lt_ref[...]
        row = lt_ref[pl.ds(j, 1), :]
        d = jnp.sum(jnp.where(lane == j, row, 0.0), axis=1, keepdims=True)
        r = lax.rsqrt(d)
        l = jnp.where(lane >= j, row * r, 0.0)
        colj = jnp.sum(jnp.where(cols == j, a, 0.0), axis=1, keepdims=True)
        c = jnp.where(sub > j, colj * r, 0.0)
        b_row = inv_ref[pl.ds(j, 1), :] * r
        lt_ref[...] = a - c * l
        inv_ref[...] = inv_ref[...] - c * b_row
        lt_ref[pl.ds(j, 1), :] = l
        inv_ref[pl.ds(j, 1), :] = b_row
        return carry

    lax.fori_loop(0, n, step, 0)


def chol_inv(g):
    n = g.shape[0]
    return pl.pallas_call(
        chol_inv_kernel,
        out_shape=(
            jax.ShapeDtypeStruct((n, n), jnp.float32),
            jax.ShapeDtypeStruct((n, n), jnp.float32),
        ),
        in_specs=[pl.BlockSpec(memory_space=pltpu.VMEM)],
        out_specs=(pl.BlockSpec(memory_space=pltpu.VMEM), pl.BlockSpec(memory_space=pltpu.VMEM)),
    )(g)


HALF_PI_HI = 1.5703125
HALF_PI_LO = 4.8382679e-04


def sin_cos(angle):
    turns = jnp.round(angle * (2.0 / math.pi))
    rest = (angle - turns * HALF_PI_HI) - turns * HALF_PI_LO
    quadrant = turns.astype(jnp.int32) & 3
    sq = rest * rest
    sine = rest + rest * sq * (-1.0 / 6 + sq * (1.0 / 120 + sq * (-1.0 / 5040 + sq * (1.0 / 362880))))
    cosine = 1.0 + sq * (-0.5 + sq * (1.0 / 24 + sq * (-1.0 / 720 + sq * (1.0 / 40320))))
    swap = (quadrant & 1) == 1
    sin_v = jnp.where(swap, cosine, sine)
    cos_v = jnp.where(swap, sine, cosine)
    sin_v = jnp.where(quadrant >= 2, -sin_v, sin_v)
    cos_v = jnp.where((quadrant == 1) | (quadrant == 2), -cos_v, cos_v)
    return sin_v, cos_v


def jacobian_planes(pixels, wave_scale, flux_level, codes, field_re, field_im):
    delta_u = pixels // FOCAL - FOCAL // 2
    delta_v = pixels % FOCAL - FOCAL // 2
    mirror = codes // (GRID * GRID)
    column_x = codes // GRID % GRID - GRID // 2
    column_y = codes % GRID - GRID // 2
    phase_int = delta_u[:, None] * column_x[None, :] + delta_v[:, None] * column_y[None, :]
    radius = (delta_u * delta_u + delta_v * delta_v).astype(jnp.float32)
    amplitude = flux_level * jnp.exp(-INFL_RATE * radius / (FOCAL * FOCAL))
    defocus = radius * (TWO_PI * DEFOCUS_RATE / (FOCAL * FOCAL)) / wave_scale
    phase_angle = mirror.astype(jnp.float32)[None, :] * defocus[
        :, None
    ] - TWO_PI / FOCAL * wave_scale * phase_int.astype(jnp.float32)
    sine_part, cosine = sin_cos(phase_angle)
    real_part = amplitude[:, None] * (field_re[None, :] * cosine - field_im[None, :] * sine_part)
    imag_part = amplitude[:, None] * (field_re[None, :] * sine_part + field_im[None, :] * cosine)
    return real_part.astype(jnp.bfloat16), imag_part.astype(jnp.bfloat16)


def gram_of(sketch):
    return lax.dot_general(
        sketch,
        sketch,
        (((0,), (0,)), ((), ())),
        precision=lax.Precision.HIGHEST,
        preferred_element_type=jnp.float32,
    )


def on_device(pixel_index, act_map, omega, pupil_field, channel_scale, channel_flux):
    pixels = pixel_index[0]
    npix = pixels.shape[0]
    rows_dev = 2 * npix
    act_count = lax.axis_size("act")
    pix_count = lax.axis_size("pix")
    total_rows = rows_dev * pix_count
    share_pix = npix // act_count
    real_rows, imag_rows = jacobian_planes(
        pixels, channel_scale[0], channel_flux[0], act_map, pupil_field[0, 0], pupil_field[0, 1]
    )
    jac = jnp.concatenate([real_rows, imag_rows], axis=0)
    partial_sketch = jnp.dot(jac, omega, preferred_element_type=jnp.float32)
    sketch = sum_by_parts(partial_sketch, "act")
    gram_matrix = butterfly_sum(gram_of(sketch), "pix")
    upper_factor, lower_inverse = chol_inv(gram_matrix)
    basis = lax.dot_general(
        sketch,
        lower_inverse,
        (((1,), (1,)), ((), ())),
        precision=lax.Precision.HIGHEST,
        preferred_element_type=jnp.float32,
    )
    first = lax.axis_index("act") * share_pix
    own_re = lax.dynamic_slice_in_dim(basis, first, share_pix, 0)
    own_im = lax.dynamic_slice_in_dim(basis, npix + first, share_pix, 0)
    own_basis = jnp.stack([own_re, own_im], axis=1).reshape(2 * share_pix, RANK)
    coarse = basis.astype(jnp.bfloat16)
    partial_value = lax.dot_general(
        coarse, jac, (((0,), (0,)), ((), ())), preferred_element_type=jnp.float32
    )
    parts = in_blocks(partial_value.astype(jnp.bfloat16), 0, pix_count)
    arrived = lax.all_to_all(parts, "pix", split_axis=0, concat_axis=0, tiled=True)
    projection = arrived.astype(jnp.float32).sum(axis=0)
    basis_out = (own_basis * math.sqrt(total_rows)).reshape(1, 2 * share_pix, RANK)
    r_factor = upper_factor / math.sqrt(total_rows * ACT)
    return (basis_out, projection, r_factor)


def solution(mesh):
    return jax.shard_map(
        on_device,
        mesh=mesh,
        in_specs=(
            P("pix", None),
            P("act"),
            P("act", None),
            P("pix", None, "act"),
            P("pix"),
            P("pix"),
        ),
        out_specs=(P("pix", "act", None), P("pix", "act"), P()),
        check_vma=False,
    )
```

```python
import math

import jax
import jax.numpy as jnp
from jax import lax
from jax.experimental import pallas as pl
from jax.experimental.pallas import tpu as pltpu
from jax.sharding import PartitionSpec as P

GRID = 128
FOCAL = 256
RANK = 128
ACT = 32768


TWO_PI = 2.0 * math.pi
INFL_RATE = 4.5
DEFOCUS_RATE = 6.0


def rows_for(lines, count):
    spare = -len(lines) % count
    return jnp.pad(lines, [(0, spare)] + [(0, 0)] * (lines.ndim - 1))


def sent_to_all(value, axis):
    copies = jnp.broadcast_to(value, (lax.axis_size(axis), *value.shape))
    return lax.all_to_all(copies, axis, split_axis=0, concat_axis=0, tiled=True)


def laid_out(parts, dim):
    shape = list(parts.shape[1:])
    shape[dim] *= parts.shape[0]
    return jnp.moveaxis(parts, 0, dim).reshape(shape)


def collect(value, axis, dim):
    parts = sent_to_all(value, axis)
    return laid_out(parts, dim)


def in_blocks(value, dim, count):
    before, after = (value.shape[:dim], value.shape[dim + 1 :])
    return jnp.moveaxis(value.reshape(*before, count, -1, *after), dim, 0)


def summed_on_arrival(value, axis, dim):
    parts = in_blocks(value, dim, lax.axis_size(axis))
    arrived = lax.all_to_all(parts, axis, split_axis=0, concat_axis=0, tiled=True)
    return arrived.sum(axis=0)


def sum_by_parts(value, axes):
    lines = value.reshape(-1, value.shape[-1])
    padded = rows_for(lines, lax.axis_size(axes))
    whole = collect(summed_on_arrival(padded, axes, 0), axes, 0)
    return lax.slice_in_dim(whole, 0, len(lines)).reshape(value.shape)


def butterfly_sum(value, axis):
    count = lax.axis_size(axis)
    step = 1
    while step < count:
        pairs = [(i, i ^ step) for i in range(count)]
        value = value + lax.ppermute(value, axis, pairs)
        step *= 2
    return value


def chol_inv_kernel(g_ref, lt_ref, inv_ref):
    n = g_ref.shape[0]
    lt_ref[...] = g_ref[...]
    rows = lax.broadcasted_iota(jnp.int32, (n, n), 0)
    cols = lax.broadcasted_iota(jnp.int32, (n, n), 1)
    inv_ref[...] = jnp.where(rows == cols, 1.0, 0.0).astype(jnp.float32)
    lane = lax.broadcasted_iota(jnp.int32, (1, n), 1)
    sub = lax.broadcasted_iota(jnp.int32, (n, 1), 0)

    def step(t, carry):
        j = 2 * t
        a_mat = lt_ref[...]
        r0 = lt_ref[pl.ds(j, 1), :]
        r1 = lt_ref[pl.ds(j + 1, 1), :]
        piv = jnp.sum(jnp.where(lane == j, r0, 0.0), axis=1, keepdims=True)
        off = jnp.sum(jnp.where(lane == j + 1, r0, 0.0), axis=1, keepdims=True)
        nxt = jnp.sum(jnp.where(lane == j + 1, r1, 0.0), axis=1, keepdims=True)
        ra = lax.rsqrt(piv)
        ratio = off * ra * ra
        rd = lax.rsqrt(piv * nxt - off * off) * (piv * ra)
        l0 = jnp.where(lane >= j, r0 * ra, 0.0)
        l1 = jnp.where(lane >= j + 1, (r1 - r0 * ratio) * rd, 0.0)
        col0 = jnp.sum(jnp.where(cols == j, a_mat, 0.0), axis=1, keepdims=True)
        col1 = jnp.sum(jnp.where(cols == j + 1, a_mat, 0.0), axis=1, keepdims=True)
        below = sub > j + 1
        c0 = jnp.where(below, col0 * ra, 0.0)
        c1 = jnp.where(below, (col1 - col0 * ratio) * rd, 0.0)
        b0 = inv_ref[pl.ds(j, 1), :] * ra
        b1 = (inv_ref[pl.ds(j + 1, 1), :] - b0 * (off * ra)) * rd
        lt_ref[...] = a_mat - c0 * l0 - c1 * l1
        inv_ref[...] = inv_ref[...] - c0 * b0 - c1 * b1
        lt_ref[pl.ds(j, 1), :] = l0
        lt_ref[pl.ds(j + 1, 1), :] = l1
        inv_ref[pl.ds(j, 1), :] = b0
        inv_ref[pl.ds(j + 1, 1), :] = b1
        return carry

    lax.fori_loop(0, n // 2, step, 0)


def chol_inv(g):
    n = g.shape[0]
    return pl.pallas_call(
        chol_inv_kernel,
        out_shape=(
            jax.ShapeDtypeStruct((n, n), jnp.float32),
            jax.ShapeDtypeStruct((n, n), jnp.float32),
        ),
        in_specs=[pl.BlockSpec(memory_space=pltpu.VMEM)],
        out_specs=(pl.BlockSpec(memory_space=pltpu.VMEM), pl.BlockSpec(memory_space=pltpu.VMEM)),
    )(g)


HALF_PI_HI = 1.5703125
HALF_PI_LO = 4.8382679e-04


def sin_cos(angle):
    turns = jnp.round(angle * (2.0 / math.pi))
    rest = (angle - turns * HALF_PI_HI) - turns * HALF_PI_LO
    quadrant = turns.astype(jnp.int32) & 3
    sq = rest * rest
    sine = rest + rest * sq * (-1.0 / 6 + sq * (1.0 / 120 + sq * (-1.0 / 5040 + sq * (1.0 / 362880))))
    cosine = 1.0 + sq * (-0.5 + sq * (1.0 / 24 + sq * (-1.0 / 720 + sq * (1.0 / 40320))))
    swap = (quadrant & 1) == 1
    sin_v = jnp.where(swap, cosine, sine)
    cos_v = jnp.where(swap, sine, cosine)
    sin_v = jnp.where(quadrant >= 2, -sin_v, sin_v)
    cos_v = jnp.where((quadrant == 1) | (quadrant == 2), -cos_v, cos_v)
    return sin_v, cos_v


def jacobian_planes(pixels, wave_scale, flux_level, codes, field_re, field_im):
    delta_u = pixels // FOCAL - FOCAL // 2
    delta_v = pixels % FOCAL - FOCAL // 2
    mirror = codes // (GRID * GRID)
    column_x = codes // GRID % GRID - GRID // 2
    column_y = codes % GRID - GRID // 2
    phase_int = delta_u[:, None] * column_x[None, :] + delta_v[:, None] * column_y[None, :]
    radius = (delta_u * delta_u + delta_v * delta_v).astype(jnp.float32)
    amplitude = flux_level * jnp.exp(-INFL_RATE * radius / (FOCAL * FOCAL))
    defocus = radius * (TWO_PI * DEFOCUS_RATE / (FOCAL * FOCAL)) / wave_scale
    phase_angle = mirror.astype(jnp.float32)[None, :] * defocus[
        :, None
    ] - TWO_PI / FOCAL * wave_scale * phase_int.astype(jnp.float32)
    sine_part, cosine = sin_cos(phase_angle)
    real_part = amplitude[:, None] * (field_re[None, :] * cosine - field_im[None, :] * sine_part)
    imag_part = amplitude[:, None] * (field_re[None, :] * sine_part + field_im[None, :] * cosine)
    return real_part.astype(jnp.bfloat16), imag_part.astype(jnp.bfloat16)


def gram_of(sketch):
    return lax.dot_general(
        sketch,
        sketch,
        (((0,), (0,)), ((), ())),
        precision=lax.Precision.HIGHEST,
        preferred_element_type=jnp.float32,
    )


def on_device(pixel_index, act_map, omega, pupil_field, channel_scale, channel_flux):
    pixels = pixel_index[0]
    npix = pixels.shape[0]
    rows_dev = 2 * npix
    act_count = lax.axis_size("act")
    pix_count = lax.axis_size("pix")
    total_rows = rows_dev * pix_count
    share_pix = npix // act_count
    real_rows, imag_rows = jacobian_planes(
        pixels, channel_scale[0], channel_flux[0], act_map, pupil_field[0, 0], pupil_field[0, 1]
    )
    jac = jnp.concatenate([real_rows, imag_rows], axis=0)
    partial_sketch = jnp.dot(jac, omega, preferred_element_type=jnp.float32)
    sketch = sum_by_parts(partial_sketch, "act")
    gram_matrix = butterfly_sum(gram_of(sketch), "pix")
    upper_factor, lower_inverse = chol_inv(gram_matrix)
    basis = lax.dot_general(
        sketch,
        lower_inverse,
        (((1,), (1,)), ((), ())),
        precision=lax.Precision.HIGHEST,
        preferred_element_type=jnp.float32,
    )
    first = lax.axis_index("act") * share_pix
    own_re = lax.dynamic_slice_in_dim(basis, first, share_pix, 0)
    own_im = lax.dynamic_slice_in_dim(basis, npix + first, share_pix, 0)
    own_basis = jnp.stack([own_re, own_im], axis=1).reshape(2 * share_pix, RANK)
    coarse = basis.astype(jnp.bfloat16)
    partial_value = lax.dot_general(
        coarse, jac, (((0,), (0,)), ((), ())), preferred_element_type=jnp.float32
    )
    parts = in_blocks(partial_value.astype(jnp.bfloat16), 0, pix_count)
    arrived = lax.all_to_all(parts, "pix", split_axis=0, concat_axis=0, tiled=True)
    projection = arrived.astype(jnp.float32).sum(axis=0)
    basis_out = (own_basis * math.sqrt(total_rows)).reshape(1, 2 * share_pix, RANK)
    r_factor = upper_factor / math.sqrt(total_rows * ACT)
    return (basis_out, projection, r_factor)


def solution(mesh):
    return jax.shard_map(
        on_device,
        mesh=mesh,
        in_specs=(
            P("pix", None),
            P("act"),
            P("act", None),
            P("pix", None, "act"),
            P("pix"),
            P("pix"),
        ),
        out_specs=(P("pix", "act", None), P("pix", "act"), P()),
        check_vma=False,
    )
```

```python
import math

import jax
import jax.numpy as jnp
from jax import lax
from jax.experimental import pallas as pl
from jax.experimental.pallas import tpu as pltpu
from jax.sharding import PartitionSpec as P

GRID = 128
FOCAL = 256
RANK = 128
ACT = 32768


TWO_PI = 2.0 * math.pi
INFL_RATE = 4.5
DEFOCUS_RATE = 6.0


def rows_for(lines, count):
    spare = -len(lines) % count
    return jnp.pad(lines, [(0, spare)] + [(0, 0)] * (lines.ndim - 1))


def sent_to_all(value, axis):
    copies = jnp.broadcast_to(value, (lax.axis_size(axis), *value.shape))
    return lax.all_to_all(copies, axis, split_axis=0, concat_axis=0, tiled=True)


def laid_out(parts, dim):
    shape = list(parts.shape[1:])
    shape[dim] *= parts.shape[0]
    return jnp.moveaxis(parts, 0, dim).reshape(shape)


def collect(value, axis, dim):
    parts = sent_to_all(value, axis)
    return laid_out(parts, dim)


def in_blocks(value, dim, count):
    before, after = (value.shape[:dim], value.shape[dim + 1 :])
    return jnp.moveaxis(value.reshape(*before, count, -1, *after), dim, 0)


def summed_on_arrival(value, axis, dim):
    parts = in_blocks(value, dim, lax.axis_size(axis))
    arrived = lax.all_to_all(parts, axis, split_axis=0, concat_axis=0, tiled=True)
    return arrived.sum(axis=0)


def sum_by_parts(value, axes):
    lines = value.reshape(-1, value.shape[-1])
    padded = rows_for(lines, lax.axis_size(axes))
    whole = collect(summed_on_arrival(padded, axes, 0), axes, 0)
    return lax.slice_in_dim(whole, 0, len(lines)).reshape(value.shape)


def butterfly_sum(value, axis):
    count = lax.axis_size(axis)
    step = 1
    while step < count:
        pairs = [(i, i ^ step) for i in range(count)]
        value = value + lax.ppermute(value, axis, pairs)
        step *= 2
    return value


STEP = 4


def chol_inv_kernel(g_ref, lt_ref, inv_ref):
    n = g_ref.shape[0]
    lt_ref[...] = g_ref[...]
    rows = lax.broadcasted_iota(jnp.int32, (n, n), 0)
    cols = lax.broadcasted_iota(jnp.int32, (n, n), 1)
    inv_ref[...] = jnp.where(rows == cols, 1.0, 0.0).astype(jnp.float32)
    lane = lax.broadcasted_iota(jnp.int32, (1, n), 1)
    sub = lax.broadcasted_iota(jnp.int32, (n, 1), 0)

    def step(t, carry):
        j = STEP * t
        a_mat = lt_ref[...]
        r = [lt_ref[pl.ds(j + i, 1), :] for i in range(STEP)]
        blk = {}
        for i in range(STEP):
            for k in range(i, STEP):
                blk[i, k] = jnp.sum(jnp.where(lane == j + k, r[i], 0.0), axis=1, keepdims=True)
        low, inv = {}, []
        for i in range(STEP):
            s = blk[i, i]
            for k in range(i):
                s = s - low[i, k] * low[i, k]
            inv.append(lax.rsqrt(s))
            for m in range(i + 1, STEP):
                v = blk[i, m]
                for k in range(i):
                    v = v - low[m, k] * low[i, k]
                low[m, i] = v * inv[i]
        below = sub >= j + STEP
        l_rows, b_rows, c_cols = [], [], []
        for i in range(STEP):
            lv = r[i]
            bv = inv_ref[pl.ds(j + i, 1), :]
            cv = jnp.sum(jnp.where(cols == j + i, a_mat, 0.0), axis=1, keepdims=True)
            for k in range(i):
                lv = lv - low[i, k] * l_rows[k]
                bv = bv - low[i, k] * b_rows[k]
                cv = cv - low[i, k] * c_cols[k]
            l_rows.append(jnp.where(lane >= j + i, lv * inv[i], 0.0))
            b_rows.append(bv * inv[i])
            c_cols.append(cv * inv[i])
        new_a = a_mat
        new_b = inv_ref[...]
        for i in range(STEP):
            c = jnp.where(below, c_cols[i], 0.0)
            new_a = new_a - c * l_rows[i]
            new_b = new_b - c * b_rows[i]
        lt_ref[...] = new_a
        inv_ref[...] = new_b
        for i in range(STEP):
            lt_ref[pl.ds(j + i, 1), :] = l_rows[i]
            inv_ref[pl.ds(j + i, 1), :] = b_rows[i]
        return carry

    lax.fori_loop(0, n // STEP, step, 0)


def chol_inv(g):
    n = g.shape[0]
    return pl.pallas_call(
        chol_inv_kernel,
        out_shape=(
            jax.ShapeDtypeStruct((n, n), jnp.float32),
            jax.ShapeDtypeStruct((n, n), jnp.float32),
        ),
        in_specs=[pl.BlockSpec(memory_space=pltpu.VMEM)],
        out_specs=(pl.BlockSpec(memory_space=pltpu.VMEM), pl.BlockSpec(memory_space=pltpu.VMEM)),
    )(g)


HALF_PI_HI = 1.5703125
HALF_PI_LO = 4.8382679e-04


def sin_cos(angle):
    turns = jnp.round(angle * (2.0 / math.pi))
    rest = (angle - turns * HALF_PI_HI) - turns * HALF_PI_LO
    quadrant = turns.astype(jnp.int32) & 3
    sq = rest * rest
    sine = rest + rest * sq * (-1.0 / 6 + sq * (1.0 / 120 + sq * (-1.0 / 5040 + sq * (1.0 / 362880))))
    cosine = 1.0 + sq * (-0.5 + sq * (1.0 / 24 + sq * (-1.0 / 720 + sq * (1.0 / 40320))))
    swap = (quadrant & 1) == 1
    sin_v = jnp.where(swap, cosine, sine)
    cos_v = jnp.where(swap, sine, cosine)
    sin_v = jnp.where(quadrant >= 2, -sin_v, sin_v)
    cos_v = jnp.where((quadrant == 1) | (quadrant == 2), -cos_v, cos_v)
    return sin_v, cos_v


def jacobian_planes(pixels, wave_scale, flux_level, codes, field_re, field_im):
    delta_u = pixels // FOCAL - FOCAL // 2
    delta_v = pixels % FOCAL - FOCAL // 2
    mirror = codes // (GRID * GRID)
    column_x = codes // GRID % GRID - GRID // 2
    column_y = codes % GRID - GRID // 2
    phase_int = delta_u[:, None] * column_x[None, :] + delta_v[:, None] * column_y[None, :]
    radius = (delta_u * delta_u + delta_v * delta_v).astype(jnp.float32)
    amplitude = flux_level * jnp.exp(-INFL_RATE * radius / (FOCAL * FOCAL))
    defocus = radius * (TWO_PI * DEFOCUS_RATE / (FOCAL * FOCAL)) / wave_scale
    phase_angle = mirror.astype(jnp.float32)[None, :] * defocus[
        :, None
    ] - TWO_PI / FOCAL * wave_scale * phase_int.astype(jnp.float32)
    sine_part, cosine = sin_cos(phase_angle)
    real_part = amplitude[:, None] * (field_re[None, :] * cosine - field_im[None, :] * sine_part)
    imag_part = amplitude[:, None] * (field_re[None, :] * sine_part + field_im[None, :] * cosine)
    return real_part.astype(jnp.bfloat16), imag_part.astype(jnp.bfloat16)


def gram_of(sketch):
    return lax.dot_general(
        sketch,
        sketch,
        (((0,), (0,)), ((), ())),
        precision=lax.Precision.HIGHEST,
        preferred_element_type=jnp.float32,
    )


def on_device(pixel_index, act_map, omega, pupil_field, channel_scale, channel_flux):
    pixels = pixel_index[0]
    npix = pixels.shape[0]
    rows_dev = 2 * npix
    act_count = lax.axis_size("act")
    pix_count = lax.axis_size("pix")
    total_rows = rows_dev * pix_count
    share_pix = npix // act_count
    real_rows, imag_rows = jacobian_planes(
        pixels, channel_scale[0], channel_flux[0], act_map, pupil_field[0, 0], pupil_field[0, 1]
    )
    jac = jnp.concatenate([real_rows, imag_rows], axis=0)
    partial_sketch = jnp.dot(jac, omega, preferred_element_type=jnp.float32)
    sketch = sum_by_parts(partial_sketch, "act")
    gram_matrix = butterfly_sum(gram_of(sketch), "pix")
    upper_factor, lower_inverse = chol_inv(gram_matrix)
    basis = lax.dot_general(
        sketch,
        lower_inverse,
        (((1,), (1,)), ((), ())),
        precision=lax.Precision.HIGHEST,
        preferred_element_type=jnp.float32,
    )
    first = lax.axis_index("act") * share_pix
    own_re = lax.dynamic_slice_in_dim(basis, first, share_pix, 0)
    own_im = lax.dynamic_slice_in_dim(basis, npix + first, share_pix, 0)
    own_basis = jnp.stack([own_re, own_im], axis=1).reshape(2 * share_pix, RANK)
    coarse = basis.astype(jnp.bfloat16)
    partial_value = lax.dot_general(
        coarse, jac, (((0,), (0,)), ((), ())), preferred_element_type=jnp.float32
    )
    parts = in_blocks(partial_value.astype(jnp.bfloat16), 0, pix_count)
    arrived = lax.all_to_all(parts, "pix", split_axis=0, concat_axis=0, tiled=True)
    projection = arrived.astype(jnp.float32).sum(axis=0)
    basis_out = (own_basis * math.sqrt(total_rows)).reshape(1, 2 * share_pix, RANK)
    r_factor = upper_factor / math.sqrt(total_rows * ACT)
    return (basis_out, projection, r_factor)


def solution(mesh):
    return jax.shard_map(
        on_device,
        mesh=mesh,
        in_specs=(
            P("pix", None),
            P("act"),
            P("act", None),
            P("pix", None, "act"),
            P("pix"),
            P("pix"),
        ),
        out_specs=(P("pix", "act", None), P("pix", "act"), P()),
        check_vma=False,
    )
```

```python
import math

import jax
import jax.numpy as jnp
from jax import lax
from jax.experimental import pallas as pl
from jax.experimental.pallas import tpu as pltpu
from jax.sharding import PartitionSpec as P

GRID = 128
FOCAL = 256
RANK = 128
ACT = 32768


TWO_PI = 2.0 * math.pi
INFL_RATE = 4.5
DEFOCUS_RATE = 6.0


def rows_for(lines, count):
    spare = -len(lines) % count
    return jnp.pad(lines, [(0, spare)] + [(0, 0)] * (lines.ndim - 1))


def sent_to_all(value, axis):
    copies = jnp.broadcast_to(value, (lax.axis_size(axis), *value.shape))
    return lax.all_to_all(copies, axis, split_axis=0, concat_axis=0, tiled=True)


def laid_out(parts, dim):
    shape = list(parts.shape[1:])
    shape[dim] *= parts.shape[0]
    return jnp.moveaxis(parts, 0, dim).reshape(shape)


def collect(value, axis, dim):
    parts = sent_to_all(value, axis)
    return laid_out(parts, dim)


def in_blocks(value, dim, count):
    before, after = (value.shape[:dim], value.shape[dim + 1 :])
    return jnp.moveaxis(value.reshape(*before, count, -1, *after), dim, 0)


def summed_on_arrival(value, axis, dim):
    parts = in_blocks(value, dim, lax.axis_size(axis))
    arrived = lax.all_to_all(parts, axis, split_axis=0, concat_axis=0, tiled=True)
    return arrived.sum(axis=0)


def sum_by_parts(value, axes):
    lines = value.reshape(-1, value.shape[-1])
    padded = rows_for(lines, lax.axis_size(axes))
    whole = collect(summed_on_arrival(padded, axes, 0), axes, 0)
    return lax.slice_in_dim(whole, 0, len(lines)).reshape(value.shape)


def butterfly_sum(value, axis):
    count = lax.axis_size(axis)
    step = 1
    while step < count:
        pairs = [(i, i ^ step) for i in range(count)]
        value = value + lax.ppermute(value, axis, pairs)
        step *= 2
    return value


STEP = 4


def chol_inv_kernel(g_ref, lt_ref, inv_ref):
    n = g_ref.shape[0]
    lt_ref[...] = g_ref[...]
    rows = lax.broadcasted_iota(jnp.int32, (n, n), 0)
    cols = lax.broadcasted_iota(jnp.int32, (n, n), 1)
    inv_ref[...] = jnp.where(rows == cols, 1.0, 0.0).astype(jnp.float32)
    lane = lax.broadcasted_iota(jnp.int32, (1, n), 1)
    sub = lax.broadcasted_iota(jnp.int32, (n, 1), 0)

    def step(t, carry):
        j = STEP * t
        a_mat = lt_ref[...]
        r = [lt_ref[pl.ds(j + i, 1), :] for i in range(STEP)]
        blk = {}
        for i in range(STEP):
            for k in range(i, STEP):
                blk[i, k] = jnp.sum(jnp.where(lane == j + k, r[i], 0.0), axis=1, keepdims=True)
        low, inv = {}, []
        for i in range(STEP):
            s = blk[i, i]
            for k in range(i):
                s = s - low[i, k] * low[i, k]
            inv.append(lax.rsqrt(s))
            for m in range(i + 1, STEP):
                v = blk[i, m]
                for k in range(i):
                    v = v - low[m, k] * low[i, k]
                low[m, i] = v * inv[i]
        below = sub >= j + STEP
        l_rows, b_rows, c_cols = [], [], []
        for i in range(STEP):
            lv = r[i]
            bv = inv_ref[pl.ds(j + i, 1), :]
            cv = jnp.sum(jnp.where(cols == j + i, a_mat, 0.0), axis=1, keepdims=True)
            for k in range(i):
                lv = lv - low[i, k] * l_rows[k]
                bv = bv - low[i, k] * b_rows[k]
                cv = cv - low[i, k] * c_cols[k]
            l_rows.append(jnp.where(lane >= j + i, lv * inv[i], 0.0))
            b_rows.append(bv * inv[i])
            c_cols.append(cv * inv[i])
        new_a = a_mat
        new_b = inv_ref[...]
        for i in range(STEP):
            c = jnp.where(below, c_cols[i], 0.0)
            new_a = new_a - c * l_rows[i]
            new_b = new_b - c * b_rows[i]
        lt_ref[...] = new_a
        inv_ref[...] = new_b
        for i in range(STEP):
            lt_ref[pl.ds(j + i, 1), :] = l_rows[i]
            inv_ref[pl.ds(j + i, 1), :] = b_rows[i]
        return carry

    lax.fori_loop(0, n // STEP, step, 0)


def chol_inv(g):
    n = g.shape[0]
    return pl.pallas_call(
        chol_inv_kernel,
        out_shape=(
            jax.ShapeDtypeStruct((n, n), jnp.float32),
            jax.ShapeDtypeStruct((n, n), jnp.float32),
        ),
        in_specs=[pl.BlockSpec(memory_space=pltpu.VMEM)],
        out_specs=(pl.BlockSpec(memory_space=pltpu.VMEM), pl.BlockSpec(memory_space=pltpu.VMEM)),
    )(g)


HALF_PI_HI = 1.5703125
HALF_PI_LO = 4.8382679e-04


def sin_cos(angle):
    turns = jnp.round(angle * (2.0 / math.pi))
    rest = (angle - turns * HALF_PI_HI) - turns * HALF_PI_LO
    quadrant = turns.astype(jnp.int32) & 3
    sq = rest * rest
    sine = rest + rest * sq * (-1.0 / 6 + sq * (1.0 / 120 + sq * (-1.0 / 5040 + sq * (1.0 / 362880))))
    cosine = 1.0 + sq * (-0.5 + sq * (1.0 / 24 + sq * (-1.0 / 720 + sq * (1.0 / 40320))))
    swap = (quadrant & 1) == 1
    sin_v = jnp.where(swap, cosine, sine)
    cos_v = jnp.where(swap, sine, cosine)
    sin_v = jnp.where(quadrant >= 2, -sin_v, sin_v)
    cos_v = jnp.where((quadrant == 1) | (quadrant == 2), -cos_v, cos_v)
    return sin_v, cos_v


def jacobian_planes(pixels, wave_scale, flux_level, codes, field_re, field_im):
    delta_u = pixels // FOCAL - FOCAL // 2
    delta_v = pixels % FOCAL - FOCAL // 2
    mirror = codes // (GRID * GRID)
    column_x = codes // GRID % GRID - GRID // 2
    column_y = codes % GRID - GRID // 2
    phase_int = delta_u[:, None] * column_x[None, :] + delta_v[:, None] * column_y[None, :]
    radius = (delta_u * delta_u + delta_v * delta_v).astype(jnp.float32)
    amplitude = flux_level * jnp.exp(-INFL_RATE * radius / (FOCAL * FOCAL))
    defocus = radius * (TWO_PI * DEFOCUS_RATE / (FOCAL * FOCAL)) / wave_scale
    phase_angle = mirror.astype(jnp.float32)[None, :] * defocus[
        :, None
    ] - TWO_PI / FOCAL * wave_scale * phase_int.astype(jnp.float32)
    sine_part, cosine = sin_cos(phase_angle)
    real_part = amplitude[:, None] * (field_re[None, :] * cosine - field_im[None, :] * sine_part)
    imag_part = amplitude[:, None] * (field_re[None, :] * sine_part + field_im[None, :] * cosine)
    return real_part.astype(jnp.bfloat16), imag_part.astype(jnp.bfloat16)


BLOCK = 64

def jac_kernel(pix_ref, code_ref, field_ref, scale_ref, flux_ref, omega_ref, jac_ref, sketch_ref):
    npix = pix_ref.shape[1]
    wave_scale = scale_ref[0]
    flux_level = flux_ref[0]
    pixels = pix_ref[...]
    delta_u = pixels // FOCAL - FOCAL // 2
    delta_v = pixels % FOCAL - FOCAL // 2
    radius = (delta_u * delta_u + delta_v * delta_v).astype(jnp.float32)
    amplitude = flux_level * jnp.exp(-INFL_RATE * radius / (FOCAL * FOCAL))
    defocus = radius * (TWO_PI * DEFOCUS_RATE / (FOCAL * FOCAL)) / wave_scale
    zero = jnp.zeros_like(radius)
    terms = jnp.concatenate(
        [delta_u.astype(jnp.float32), delta_v.astype(jnp.float32), amplitude, defocus, zero, zero, zero, zero], axis=0
    ).T
    codes = code_ref[...]
    mirror = (codes // (GRID * GRID)).astype(jnp.float32)
    col_x = (codes // GRID % GRID - GRID // 2).astype(jnp.float32)
    col_y = (codes % GRID - GRID // 2).astype(jnp.float32)
    e_re = field_ref[0:1, :]
    e_im = field_ref[1:2, :]
    rate = TWO_PI / FOCAL * wave_scale
    for b in range(npix // BLOCK):
        t = terms[b * BLOCK : (b + 1) * BLOCK]
        du, dv, amp, defo = t[:, 0:1], t[:, 1:2], t[:, 2:3], t[:, 3:4]
        phase = mirror * defo - rate * (du * col_x + dv * col_y)
        sine, cosine = sin_cos(phase)
        jac_ref[b * BLOCK : (b + 1) * BLOCK, :] = (amp * (e_re * cosine - e_im * sine)).astype(jnp.bfloat16)
        jac_ref[npix + b * BLOCK : npix + (b + 1) * BLOCK, :] = (amp * (e_re * sine + e_im * cosine)).astype(jnp.bfloat16)
    sketch_ref[...] = jnp.dot(jac_ref[...], omega_ref[...], preferred_element_type=jnp.float32)

def jac_and_sketch(pixel_row, codes_row, field, scale, flux, omega):
    npix = pixel_row.shape[1]; nact = codes_row.shape[1]
    vm = pl.BlockSpec(memory_space=pltpu.VMEM)
    return pl.pallas_call(
        jac_kernel,
        out_shape=(jax.ShapeDtypeStruct((2 * npix, nact), jnp.bfloat16), jax.ShapeDtypeStruct((2 * npix, omega.shape[1]), jnp.float32)),
        in_specs=[vm, vm, vm, pl.BlockSpec(memory_space=pltpu.SMEM), pl.BlockSpec(memory_space=pltpu.SMEM), vm],
        out_specs=(vm, vm),
    )(pixel_row, codes_row, field, scale, flux, omega)


def gram_of(sketch):
    return lax.dot_general(
        sketch,
        sketch,
        (((0,), (0,)), ((), ())),
        precision=lax.Precision.HIGHEST,
        preferred_element_type=jnp.float32,
    )


def on_device(pixel_index, act_map, omega, pupil_field, channel_scale, channel_flux):
    pixels = pixel_index[0]
    npix = pixels.shape[0]
    rows_dev = 2 * npix
    act_count = lax.axis_size("act")
    pix_count = lax.axis_size("pix")
    total_rows = rows_dev * pix_count
    share_pix = npix // act_count
    jac, partial_sketch = jac_and_sketch(
        pixel_index, act_map[None, :], pupil_field[0], channel_scale, channel_flux, omega
    )
    sketch = sum_by_parts(partial_sketch, "act")
    gram_matrix = butterfly_sum(gram_of(sketch), "pix")
    upper_factor, lower_inverse = chol_inv(gram_matrix)
    basis = lax.dot_general(
        sketch,
        lower_inverse,
        (((1,), (1,)), ((), ())),
        precision=lax.Precision.HIGHEST,
        preferred_element_type=jnp.float32,
    )
    first = lax.axis_index("act") * share_pix
    own_re = lax.dynamic_slice_in_dim(basis, first, share_pix, 0)
    own_im = lax.dynamic_slice_in_dim(basis, npix + first, share_pix, 0)
    own_basis = jnp.stack([own_re, own_im], axis=1).reshape(2 * share_pix, RANK)
    coarse = basis.astype(jnp.bfloat16)
    partial_value = lax.dot_general(
        coarse, jac, (((0,), (0,)), ((), ())), preferred_element_type=jnp.float32
    )
    parts = in_blocks(partial_value.astype(jnp.bfloat16), 0, pix_count)
    arrived = lax.all_to_all(parts, "pix", split_axis=0, concat_axis=0, tiled=True)
    projection = arrived.astype(jnp.float32).sum(axis=0)
    basis_out = (own_basis * math.sqrt(total_rows)).reshape(1, 2 * share_pix, RANK)
    r_factor = upper_factor / math.sqrt(total_rows * ACT)
    return (basis_out, projection, r_factor)


def solution(mesh):
    return jax.shard_map(
        on_device,
        mesh=mesh,
        in_specs=(
            P("pix", None),
            P("act"),
            P("act", None),
            P("pix", None, "act"),
            P("pix"),
            P("pix"),
        ),
        out_specs=(P("pix", "act", None), P("pix", "act"), P()),
        check_vma=False,
    )
```

```python
import math

import jax
import jax.numpy as jnp
from jax import lax
from jax.experimental import pallas as pl
from jax.experimental.pallas import tpu as pltpu
from jax.sharding import PartitionSpec as P

GRID = 128
FOCAL = 256
RANK = 128
ACT = 32768


TWO_PI = 2.0 * math.pi
INFL_RATE = 4.5
DEFOCUS_RATE = 6.0


def rows_for(lines, count):
    spare = -len(lines) % count
    return jnp.pad(lines, [(0, spare)] + [(0, 0)] * (lines.ndim - 1))


def sent_to_all(value, axis):
    copies = jnp.broadcast_to(value, (lax.axis_size(axis), *value.shape))
    return lax.all_to_all(copies, axis, split_axis=0, concat_axis=0, tiled=True)


def laid_out(parts, dim):
    shape = list(parts.shape[1:])
    shape[dim] *= parts.shape[0]
    return jnp.moveaxis(parts, 0, dim).reshape(shape)


def collect(value, axis, dim):
    parts = sent_to_all(value, axis)
    return laid_out(parts, dim)


def in_blocks(value, dim, count):
    before, after = (value.shape[:dim], value.shape[dim + 1 :])
    return jnp.moveaxis(value.reshape(*before, count, -1, *after), dim, 0)


def summed_on_arrival(value, axis, dim):
    parts = in_blocks(value, dim, lax.axis_size(axis))
    arrived = lax.all_to_all(parts, axis, split_axis=0, concat_axis=0, tiled=True)
    return arrived.sum(axis=0)


def sum_by_parts(value, axes):
    lines = value.reshape(-1, value.shape[-1])
    padded = rows_for(lines, lax.axis_size(axes))
    whole = collect(summed_on_arrival(padded, axes, 0), axes, 0)
    return lax.slice_in_dim(whole, 0, len(lines)).reshape(value.shape)


def paired_sum(value, axis):
    count = lax.axis_size(axis)
    pair = value + lax.ppermute(value, axis, [(i, i ^ 1) for i in range(count)])
    pairs = count // 2
    got = [pair] + [
        lax.ppermute(pair, axis, [(i, i ^ (2 * m)) for i in range(count)]) for m in range(1, pairs)
    ]
    mine = lax.axis_index(axis) // 2
    total = None
    for q in range(pairs):
        term = sum(jnp.where((mine ^ m) == q, got[m], 0.0) for m in range(pairs))
        total = term if total is None else total + term
    return total


def butterfly_sum(value, axis):
    count = lax.axis_size(axis)
    step = 1
    while step < count:
        pairs = [(i, i ^ step) for i in range(count)]
        value = value + lax.ppermute(value, axis, pairs)
        step *= 2
    return value


STEP = 4


def chol_inv_kernel(g_ref, lt_ref, inv_ref):
    n = g_ref.shape[0]
    lt_ref[...] = g_ref[...]
    rows = lax.broadcasted_iota(jnp.int32, (n, n), 0)
    cols = lax.broadcasted_iota(jnp.int32, (n, n), 1)
    inv_ref[...] = jnp.where(rows == cols, 1.0, 0.0).astype(jnp.float32)
    lane = lax.broadcasted_iota(jnp.int32, (1, n), 1)
    sub = lax.broadcasted_iota(jnp.int32, (n, 1), 0)

    def step(t, carry):
        j = STEP * t
        a_mat = lt_ref[...]
        r = [lt_ref[pl.ds(j + i, 1), :] for i in range(STEP)]
        blk = {}
        for i in range(STEP):
            for k in range(i, STEP):
                blk[i, k] = jnp.sum(jnp.where(lane == j + k, r[i], 0.0), axis=1, keepdims=True)
        low, inv = {}, []
        for i in range(STEP):
            s = blk[i, i]
            for k in range(i):
                s = s - low[i, k] * low[i, k]
            inv.append(lax.rsqrt(s))
            for m in range(i + 1, STEP):
                v = blk[i, m]
                for k in range(i):
                    v = v - low[m, k] * low[i, k]
                low[m, i] = v * inv[i]
        below = sub >= j + STEP
        l_rows, b_rows, c_cols = [], [], []
        for i in range(STEP):
            lv = r[i]
            bv = inv_ref[pl.ds(j + i, 1), :]
            cv = jnp.sum(jnp.where(cols == j + i, a_mat, 0.0), axis=1, keepdims=True)
            for k in range(i):
                lv = lv - low[i, k] * l_rows[k]
                bv = bv - low[i, k] * b_rows[k]
                cv = cv - low[i, k] * c_cols[k]
            l_rows.append(jnp.where(lane >= j + i, lv * inv[i], 0.0))
            b_rows.append(bv * inv[i])
            c_cols.append(cv * inv[i])
        new_a = a_mat
        new_b = inv_ref[...]
        for i in range(STEP):
            c = jnp.where(below, c_cols[i], 0.0)
            new_a = new_a - c * l_rows[i]
            new_b = new_b - c * b_rows[i]
        lt_ref[...] = new_a
        inv_ref[...] = new_b
        for i in range(STEP):
            lt_ref[pl.ds(j + i, 1), :] = l_rows[i]
            inv_ref[pl.ds(j + i, 1), :] = b_rows[i]
        return carry

    lax.fori_loop(0, n // STEP, step, 0)


def chol_inv(g):
    n = g.shape[0]
    return pl.pallas_call(
        chol_inv_kernel,
        out_shape=(
            jax.ShapeDtypeStruct((n, n), jnp.float32),
            jax.ShapeDtypeStruct((n, n), jnp.float32),
        ),
        in_specs=[pl.BlockSpec(memory_space=pltpu.VMEM)],
        out_specs=(pl.BlockSpec(memory_space=pltpu.VMEM), pl.BlockSpec(memory_space=pltpu.VMEM)),
    )(g)


HALF_PI_HI = 1.5703125
HALF_PI_LO = 4.8382679e-04


def sin_cos(angle):
    turns = jnp.round(angle * (2.0 / math.pi))
    rest = (angle - turns * HALF_PI_HI) - turns * HALF_PI_LO
    quadrant = turns.astype(jnp.int32) & 3
    sq = rest * rest
    sine = rest + rest * sq * (-1.0 / 6 + sq * (1.0 / 120 + sq * (-1.0 / 5040 + sq * (1.0 / 362880))))
    cosine = 1.0 + sq * (-0.5 + sq * (1.0 / 24 + sq * (-1.0 / 720 + sq * (1.0 / 40320))))
    swap = (quadrant & 1) == 1
    sin_v = jnp.where(swap, cosine, sine)
    cos_v = jnp.where(swap, sine, cosine)
    sin_v = jnp.where(quadrant >= 2, -sin_v, sin_v)
    cos_v = jnp.where((quadrant == 1) | (quadrant == 2), -cos_v, cos_v)
    return sin_v, cos_v


def jacobian_planes(pixels, wave_scale, flux_level, codes, field_re, field_im):
    delta_u = pixels // FOCAL - FOCAL // 2
    delta_v = pixels % FOCAL - FOCAL // 2
    mirror = codes // (GRID * GRID)
    column_x = codes // GRID % GRID - GRID // 2
    column_y = codes % GRID - GRID // 2
    phase_int = delta_u[:, None] * column_x[None, :] + delta_v[:, None] * column_y[None, :]
    radius = (delta_u * delta_u + delta_v * delta_v).astype(jnp.float32)
    amplitude = flux_level * jnp.exp(-INFL_RATE * radius / (FOCAL * FOCAL))
    defocus = radius * (TWO_PI * DEFOCUS_RATE / (FOCAL * FOCAL)) / wave_scale
    phase_angle = mirror.astype(jnp.float32)[None, :] * defocus[
        :, None
    ] - TWO_PI / FOCAL * wave_scale * phase_int.astype(jnp.float32)
    sine_part, cosine = sin_cos(phase_angle)
    real_part = amplitude[:, None] * (field_re[None, :] * cosine - field_im[None, :] * sine_part)
    imag_part = amplitude[:, None] * (field_re[None, :] * sine_part + field_im[None, :] * cosine)
    return real_part.astype(jnp.bfloat16), imag_part.astype(jnp.bfloat16)


BLOCK = 64

def jac_kernel(pix_ref, code_ref, field_ref, scale_ref, flux_ref, omega_ref, jac_ref, sketch_ref):
    npix = pix_ref.shape[1]
    wave_scale = scale_ref[0]
    flux_level = flux_ref[0]
    pixels = pix_ref[...]
    delta_u = pixels // FOCAL - FOCAL // 2
    delta_v = pixels % FOCAL - FOCAL // 2
    radius = (delta_u * delta_u + delta_v * delta_v).astype(jnp.float32)
    amplitude = flux_level * jnp.exp(-INFL_RATE * radius / (FOCAL * FOCAL))
    defocus = radius * (TWO_PI * DEFOCUS_RATE / (FOCAL * FOCAL)) / wave_scale
    zero = jnp.zeros_like(radius)
    terms = jnp.concatenate(
        [delta_u.astype(jnp.float32), delta_v.astype(jnp.float32), amplitude, defocus, zero, zero, zero, zero], axis=0
    ).T
    codes = code_ref[...]
    mirror = (codes // (GRID * GRID)).astype(jnp.float32)
    col_x = (codes // GRID % GRID - GRID // 2).astype(jnp.float32)
    col_y = (codes % GRID - GRID // 2).astype(jnp.float32)
    e_re = field_ref[0:1, :]
    e_im = field_ref[1:2, :]
    rate = TWO_PI / FOCAL * wave_scale
    for b in range(npix // BLOCK):
        t = terms[b * BLOCK : (b + 1) * BLOCK]
        du, dv, amp, defo = t[:, 0:1], t[:, 1:2], t[:, 2:3], t[:, 3:4]
        phase = mirror * defo - rate * (du * col_x + dv * col_y)
        sine, cosine = sin_cos(phase)
        jac_ref[b * BLOCK : (b + 1) * BLOCK, :] = (amp * (e_re * cosine - e_im * sine)).astype(jnp.bfloat16)
        jac_ref[npix + b * BLOCK : npix + (b + 1) * BLOCK, :] = (amp * (e_re * sine + e_im * cosine)).astype(jnp.bfloat16)
    sketch_ref[...] = jnp.dot(jac_ref[...], omega_ref[...], preferred_element_type=jnp.float32)

def jac_and_sketch(pixel_row, codes_row, field, scale, flux, omega):
    npix = pixel_row.shape[1]; nact = codes_row.shape[1]
    vm = pl.BlockSpec(memory_space=pltpu.VMEM)
    return pl.pallas_call(
        jac_kernel,
        out_shape=(jax.ShapeDtypeStruct((2 * npix, nact), jnp.bfloat16), jax.ShapeDtypeStruct((2 * npix, omega.shape[1]), jnp.float32)),
        in_specs=[vm, vm, vm, pl.BlockSpec(memory_space=pltpu.SMEM), pl.BlockSpec(memory_space=pltpu.SMEM), vm],
        out_specs=(vm, vm),
    )(pixel_row, codes_row, field, scale, flux, omega)


def gram_of(sketch):
    return lax.dot_general(
        sketch,
        sketch,
        (((0,), (0,)), ((), ())),
        precision=lax.Precision.HIGHEST,
        preferred_element_type=jnp.float32,
    )


def on_device(pixel_index, act_map, omega, pupil_field, channel_scale, channel_flux):
    pixels = pixel_index[0]
    npix = pixels.shape[0]
    rows_dev = 2 * npix
    act_count = lax.axis_size("act")
    pix_count = lax.axis_size("pix")
    total_rows = rows_dev * pix_count
    share_pix = npix // act_count
    jac, partial_sketch = jac_and_sketch(
        pixel_index, act_map[None, :], pupil_field[0], channel_scale, channel_flux, omega
    )
    sketch = sum_by_parts(partial_sketch, "act")
    gram_matrix = paired_sum(gram_of(sketch), "pix")
    upper_factor, lower_inverse = chol_inv(gram_matrix)
    basis = lax.dot_general(
        sketch,
        lower_inverse,
        (((1,), (1,)), ((), ())),
        precision=lax.Precision.HIGHEST,
        preferred_element_type=jnp.float32,
    )
    first = lax.axis_index("act") * share_pix
    own_re = lax.dynamic_slice_in_dim(basis, first, share_pix, 0)
    own_im = lax.dynamic_slice_in_dim(basis, npix + first, share_pix, 0)
    own_basis = jnp.stack([own_re, own_im], axis=1).reshape(2 * share_pix, RANK)
    coarse = basis.astype(jnp.bfloat16)
    partial_value = lax.dot_general(
        coarse, jac, (((0,), (0,)), ((), ())), preferred_element_type=jnp.float32
    )
    parts = in_blocks(partial_value.astype(jnp.bfloat16), 0, pix_count)
    arrived = lax.all_to_all(parts, "pix", split_axis=0, concat_axis=0, tiled=True)
    projection = arrived.astype(jnp.float32).sum(axis=0)
    basis_out = (own_basis * math.sqrt(total_rows)).reshape(1, 2 * share_pix, RANK)
    r_factor = upper_factor / math.sqrt(total_rows * ACT)
    return (basis_out, projection, r_factor)


def solution(mesh):
    return jax.shard_map(
        on_device,
        mesh=mesh,
        in_specs=(
            P("pix", None),
            P("act"),
            P("act", None),
            P("pix", None, "act"),
            P("pix"),
            P("pix"),
        ),
        out_specs=(P("pix", "act", None), P("pix", "act"), P()),
        check_vma=False,
    )
```

```python
import functools
import math

import jax
import jax.numpy as jnp
from jax import lax
from jax.experimental import pallas as pl
from jax.experimental.pallas import tpu as pltpu
from jax.sharding import PartitionSpec as P

GRID = 128
FOCAL = 256
RANK = 128
ACT = 32768


TWO_PI = 2.0 * math.pi
INFL_RATE = 4.5
DEFOCUS_RATE = 6.0


def rows_for(lines, count):
    spare = -len(lines) % count
    return jnp.pad(lines, [(0, spare)] + [(0, 0)] * (lines.ndim - 1))


def sent_to_all(value, axis):
    copies = jnp.broadcast_to(value, (lax.axis_size(axis), *value.shape))
    return lax.all_to_all(copies, axis, split_axis=0, concat_axis=0, tiled=True)


def laid_out(parts, dim):
    shape = list(parts.shape[1:])
    shape[dim] *= parts.shape[0]
    return jnp.moveaxis(parts, 0, dim).reshape(shape)


def collect(value, axis, dim):
    parts = sent_to_all(value, axis)
    return laid_out(parts, dim)


def in_blocks(value, dim, count):
    before, after = (value.shape[:dim], value.shape[dim + 1 :])
    return jnp.moveaxis(value.reshape(*before, count, -1, *after), dim, 0)


def summed_on_arrival(value, axis, dim):
    parts = in_blocks(value, dim, lax.axis_size(axis))
    arrived = lax.all_to_all(parts, axis, split_axis=0, concat_axis=0, tiled=True)
    return arrived.sum(axis=0)


def sum_by_parts(value, axes):
    lines = value.reshape(-1, value.shape[-1])
    padded = rows_for(lines, lax.axis_size(axes))
    whole = collect(summed_on_arrival(padded, axes, 0), axes, 0)
    return lax.slice_in_dim(whole, 0, len(lines)).reshape(value.shape)


def pair_sums(value, axis):
    count = lax.axis_size(axis)
    pair = value + lax.ppermute(value, axis, [(i, i ^ 1) for i in range(count)])
    return [pair] + [
        lax.ppermute(pair, axis, [(i, i ^ (2 * m)) for i in range(count)]) for m in range(1, count // 2)
    ]


def butterfly_sum(value, axis):
    count = lax.axis_size(axis)
    step = 1
    while step < count:
        pairs = [(i, i ^ step) for i in range(count)]
        value = value + lax.ppermute(value, axis, pairs)
        step *= 2
    return value


STEP = 4


def chol_inv_kernel(axis, *refs):
    *got, lt_ref, inv_ref = refs
    pairs = len(got)
    mine = lax.axis_index(axis) // 2
    total = None
    for q in range(pairs):
        which = mine ^ q
        term = got[pairs - 1][...]
        for k in reversed(range(pairs - 1)):
            term = jnp.where(which == k, got[k][...], term)
        total = term if total is None else total + term
    n = total.shape[0]
    lt_ref[...] = total
    rows = lax.broadcasted_iota(jnp.int32, (n, n), 0)
    cols = lax.broadcasted_iota(jnp.int32, (n, n), 1)
    inv_ref[...] = jnp.where(rows == cols, 1.0, 0.0).astype(jnp.float32)
    lane = lax.broadcasted_iota(jnp.int32, (1, n), 1)
    sub = lax.broadcasted_iota(jnp.int32, (n, 1), 0)

    def step(t, carry):
        j = STEP * t
        a_mat = lt_ref[...]
        r = [lt_ref[pl.ds(j + i, 1), :] for i in range(STEP)]
        blk = {}
        for i in range(STEP):
            for k in range(i, STEP):
                blk[i, k] = jnp.sum(jnp.where(lane == j + k, r[i], 0.0), axis=1, keepdims=True)
        low, inv = {}, []
        for i in range(STEP):
            s = blk[i, i]
            for k in range(i):
                s = s - low[i, k] * low[i, k]
            inv.append(lax.rsqrt(s))
            for m in range(i + 1, STEP):
                v = blk[i, m]
                for k in range(i):
                    v = v - low[m, k] * low[i, k]
                low[m, i] = v * inv[i]
        below = sub >= j + STEP
        l_rows, b_rows, c_cols = [], [], []
        for i in range(STEP):
            lv = r[i]
            bv = inv_ref[pl.ds(j + i, 1), :]
            cv = jnp.sum(jnp.where(cols == j + i, a_mat, 0.0), axis=1, keepdims=True)
            for k in range(i):
                lv = lv - low[i, k] * l_rows[k]
                bv = bv - low[i, k] * b_rows[k]
                cv = cv - low[i, k] * c_cols[k]
            l_rows.append(jnp.where(lane >= j + i, lv * inv[i], 0.0))
            b_rows.append(bv * inv[i])
            c_cols.append(cv * inv[i])
        new_a = a_mat
        new_b = inv_ref[...]
        for i in range(STEP):
            c = jnp.where(below, c_cols[i], 0.0)
            new_a = new_a - c * l_rows[i]
            new_b = new_b - c * b_rows[i]
        lt_ref[...] = new_a
        inv_ref[...] = new_b
        for i in range(STEP):
            lt_ref[pl.ds(j + i, 1), :] = l_rows[i]
            inv_ref[pl.ds(j + i, 1), :] = b_rows[i]
        return carry

    lax.fori_loop(0, n // STEP, step, 0)


def chol_inv(got, axis):
    n = got[0].shape[0]
    return pl.pallas_call(
        functools.partial(chol_inv_kernel, axis),
        out_shape=(
            jax.ShapeDtypeStruct((n, n), jnp.float32),
            jax.ShapeDtypeStruct((n, n), jnp.float32),
        ),
        in_specs=[pl.BlockSpec(memory_space=pltpu.VMEM)] * len(got),
        out_specs=(pl.BlockSpec(memory_space=pltpu.VMEM), pl.BlockSpec(memory_space=pltpu.VMEM)),
    )(*got)


HALF_PI_HI = 1.5703125
HALF_PI_LO = 4.8382679e-04


def sin_cos(angle):
    turns = jnp.round(angle * (2.0 / math.pi))
    rest = (angle - turns * HALF_PI_HI) - turns * HALF_PI_LO
    quadrant = turns.astype(jnp.int32) & 3
    sq = rest * rest
    sine = rest + rest * sq * (-1.0 / 6 + sq * (1.0 / 120 + sq * (-1.0 / 5040 + sq * (1.0 / 362880))))
    cosine = 1.0 + sq * (-0.5 + sq * (1.0 / 24 + sq * (-1.0 / 720 + sq * (1.0 / 40320))))
    swap = (quadrant & 1) == 1
    sin_v = jnp.where(swap, cosine, sine)
    cos_v = jnp.where(swap, sine, cosine)
    sin_v = jnp.where(quadrant >= 2, -sin_v, sin_v)
    cos_v = jnp.where((quadrant == 1) | (quadrant == 2), -cos_v, cos_v)
    return sin_v, cos_v


def jacobian_planes(pixels, wave_scale, flux_level, codes, field_re, field_im):
    delta_u = pixels // FOCAL - FOCAL // 2
    delta_v = pixels % FOCAL - FOCAL // 2
    mirror = codes // (GRID * GRID)
    column_x = codes // GRID % GRID - GRID // 2
    column_y = codes % GRID - GRID // 2
    phase_int = delta_u[:, None] * column_x[None, :] + delta_v[:, None] * column_y[None, :]
    radius = (delta_u * delta_u + delta_v * delta_v).astype(jnp.float32)
    amplitude = flux_level * jnp.exp(-INFL_RATE * radius / (FOCAL * FOCAL))
    defocus = radius * (TWO_PI * DEFOCUS_RATE / (FOCAL * FOCAL)) / wave_scale
    phase_angle = mirror.astype(jnp.float32)[None, :] * defocus[
        :, None
    ] - TWO_PI / FOCAL * wave_scale * phase_int.astype(jnp.float32)
    sine_part, cosine = sin_cos(phase_angle)
    real_part = amplitude[:, None] * (field_re[None, :] * cosine - field_im[None, :] * sine_part)
    imag_part = amplitude[:, None] * (field_re[None, :] * sine_part + field_im[None, :] * cosine)
    return real_part.astype(jnp.bfloat16), imag_part.astype(jnp.bfloat16)


BLOCK = 64

def jac_kernel(pix_ref, code_ref, field_ref, scale_ref, flux_ref, omega_ref, jac_ref, sketch_ref):
    npix = pix_ref.shape[1]
    wave_scale = scale_ref[0]
    flux_level = flux_ref[0]
    pixels = pix_ref[...]
    delta_u = pixels // FOCAL - FOCAL // 2
    delta_v = pixels % FOCAL - FOCAL // 2
    radius = (delta_u * delta_u + delta_v * delta_v).astype(jnp.float32)
    amplitude = flux_level * jnp.exp(-INFL_RATE * radius / (FOCAL * FOCAL))
    defocus = radius * (TWO_PI * DEFOCUS_RATE / (FOCAL * FOCAL)) / wave_scale
    zero = jnp.zeros_like(radius)
    terms = jnp.concatenate(
        [delta_u.astype(jnp.float32), delta_v.astype(jnp.float32), amplitude, defocus, zero, zero, zero, zero], axis=0
    ).T
    codes = code_ref[...]
    mirror = (codes // (GRID * GRID)).astype(jnp.float32)
    col_x = (codes // GRID % GRID - GRID // 2).astype(jnp.float32)
    col_y = (codes % GRID - GRID // 2).astype(jnp.float32)
    e_re = field_ref[0:1, :]
    e_im = field_ref[1:2, :]
    rate = TWO_PI / FOCAL * wave_scale
    for b in range(npix // BLOCK):
        t = terms[b * BLOCK : (b + 1) * BLOCK]
        du, dv, amp, defo = t[:, 0:1], t[:, 1:2], t[:, 2:3], t[:, 3:4]
        phase = mirror * defo - rate * (du * col_x + dv * col_y)
        sine, cosine = sin_cos(phase)
        jac_ref[b * BLOCK : (b + 1) * BLOCK, :] = (amp * (e_re * cosine - e_im * sine)).astype(jnp.bfloat16)
        jac_ref[npix + b * BLOCK : npix + (b + 1) * BLOCK, :] = (amp * (e_re * sine + e_im * cosine)).astype(jnp.bfloat16)
    sketch_ref[...] = jnp.dot(jac_ref[...], omega_ref[...], preferred_element_type=jnp.float32)

def jac_and_sketch(pixel_row, codes_row, field, scale, flux, omega):
    npix = pixel_row.shape[1]; nact = codes_row.shape[1]
    vm = pl.BlockSpec(memory_space=pltpu.VMEM)
    return pl.pallas_call(
        jac_kernel,
        out_shape=(jax.ShapeDtypeStruct((2 * npix, nact), jnp.bfloat16), jax.ShapeDtypeStruct((2 * npix, omega.shape[1]), jnp.float32)),
        in_specs=[vm, vm, vm, pl.BlockSpec(memory_space=pltpu.SMEM), pl.BlockSpec(memory_space=pltpu.SMEM), vm],
        out_specs=(vm, vm),
    )(pixel_row, codes_row, field, scale, flux, omega)


def gram_of(sketch):
    return lax.dot_general(
        sketch,
        sketch,
        (((0,), (0,)), ((), ())),
        precision=lax.Precision.HIGHEST,
        preferred_element_type=jnp.float32,
    )


def on_device(pixel_index, act_map, omega, pupil_field, channel_scale, channel_flux):
    pixels = pixel_index[0]
    npix = pixels.shape[0]
    rows_dev = 2 * npix
    act_count = lax.axis_size("act")
    pix_count = lax.axis_size("pix")
    total_rows = rows_dev * pix_count
    share_pix = npix // act_count
    jac, partial_sketch = jac_and_sketch(
        pixel_index, act_map[None, :], pupil_field[0], channel_scale, channel_flux, omega
    )
    sketch = sum_by_parts(partial_sketch, "act")
    upper_factor, lower_inverse = chol_inv(pair_sums(gram_of(sketch), "pix"), "pix")
    basis = lax.dot_general(
        sketch,
        lower_inverse,
        (((1,), (1,)), ((), ())),
        precision=lax.Precision.HIGHEST,
        preferred_element_type=jnp.float32,
    )
    first = lax.axis_index("act") * share_pix
    own_re = lax.dynamic_slice_in_dim(basis, first, share_pix, 0)
    own_im = lax.dynamic_slice_in_dim(basis, npix + first, share_pix, 0)
    own_basis = jnp.stack([own_re, own_im], axis=1).reshape(2 * share_pix, RANK)
    coarse = basis.astype(jnp.bfloat16)
    partial_value = lax.dot_general(
        coarse, jac, (((0,), (0,)), ((), ())), preferred_element_type=jnp.float32
    )
    parts = in_blocks(partial_value.astype(jnp.bfloat16), 0, pix_count)
    arrived = lax.all_to_all(parts, "pix", split_axis=0, concat_axis=0, tiled=True)
    projection = arrived.astype(jnp.float32).sum(axis=0)
    basis_out = (own_basis * math.sqrt(total_rows)).reshape(1, 2 * share_pix, RANK)
    r_factor = upper_factor / math.sqrt(total_rows * ACT)
    return (basis_out, projection, r_factor)


def solution(mesh):
    return jax.shard_map(
        on_device,
        mesh=mesh,
        in_specs=(
            P("pix", None),
            P("act"),
            P("act", None),
            P("pix", None, "act"),
            P("pix"),
            P("pix"),
        ),
        out_specs=(P("pix", "act", None), P("pix", "act"), P()),
        check_vma=False,
    )
```

```python
import math

import jax
import jax.numpy as jnp
from jax import lax
from jax.experimental import pallas as pl
from jax.experimental.pallas import tpu as pltpu
from jax.sharding import PartitionSpec as P

GRID = 128
FOCAL = 256
RANK = 128
ACT = 32768


TWO_PI = 2.0 * math.pi
INFL_RATE = 4.5
DEFOCUS_RATE = 6.0


def rows_for(lines, count):
    spare = -len(lines) % count
    return jnp.pad(lines, [(0, spare)] + [(0, 0)] * (lines.ndim - 1))


def sent_to_all(value, axis):
    copies = jnp.broadcast_to(value, (lax.axis_size(axis), *value.shape))
    return lax.all_to_all(copies, axis, split_axis=0, concat_axis=0, tiled=True)


def laid_out(parts, dim):
    shape = list(parts.shape[1:])
    shape[dim] *= parts.shape[0]
    return jnp.moveaxis(parts, 0, dim).reshape(shape)


def collect(value, axis, dim):
    parts = sent_to_all(value, axis)
    return laid_out(parts, dim)


def in_blocks(value, dim, count):
    before, after = (value.shape[:dim], value.shape[dim + 1 :])
    return jnp.moveaxis(value.reshape(*before, count, -1, *after), dim, 0)


def summed_on_arrival(value, axis, dim):
    parts = in_blocks(value, dim, lax.axis_size(axis))
    arrived = lax.all_to_all(parts, axis, split_axis=0, concat_axis=0, tiled=True)
    return arrived.sum(axis=0)


def sum_by_parts(value, axes):
    lines = value.reshape(-1, value.shape[-1])
    padded = rows_for(lines, lax.axis_size(axes))
    whole = collect(summed_on_arrival(padded, axes, 0), axes, 0)
    return lax.slice_in_dim(whole, 0, len(lines)).reshape(value.shape)


def paired_sum(value, axis):
    count = lax.axis_size(axis)
    pair = value + lax.ppermute(value, axis, [(i, i ^ 1) for i in range(count)])
    pairs = count // 2
    got = [pair] + [
        lax.ppermute(pair, axis, [(i, i ^ (2 * m)) for i in range(count)]) for m in range(1, pairs)
    ]
    mine = lax.axis_index(axis) // 2
    total = None
    for q in range(pairs):
        term = sum(jnp.where((mine ^ m) == q, got[m], 0.0) for m in range(pairs))
        total = term if total is None else total + term
    return total


def butterfly_sum(value, axis):
    count = lax.axis_size(axis)
    step = 1
    while step < count:
        pairs = [(i, i ^ step) for i in range(count)]
        value = value + lax.ppermute(value, axis, pairs)
        step *= 2
    return value


STEP = 4


def chol_inv_kernel(g_ref, lt_ref, inv_ref):
    n = g_ref.shape[0]
    lt_ref[...] = g_ref[...]
    rows = lax.broadcasted_iota(jnp.int32, (n, n), 0)
    cols = lax.broadcasted_iota(jnp.int32, (n, n), 1)
    inv_ref[...] = jnp.where(rows == cols, 1.0, 0.0).astype(jnp.float32)
    lane = lax.broadcasted_iota(jnp.int32, (1, n), 1)
    sub = lax.broadcasted_iota(jnp.int32, (n, 1), 0)

    def step(t, carry):
        j = STEP * t
        a_mat = lt_ref[...]
        r = [lt_ref[pl.ds(j + i, 1), :] for i in range(STEP)]
        blk = {}
        for i in range(STEP):
            for k in range(i, STEP):
                blk[i, k] = jnp.sum(jnp.where(lane == j + k, r[i], 0.0), axis=1, keepdims=True)
        low, inv = {}, []
        for i in range(STEP):
            s = blk[i, i]
            for k in range(i):
                s = s - low[i, k] * low[i, k]
            inv.append(lax.rsqrt(s))
            for m in range(i + 1, STEP):
                v = blk[i, m]
                for k in range(i):
                    v = v - low[m, k] * low[i, k]
                low[m, i] = v * inv[i]
        below = sub >= j + STEP
        l_rows, b_rows, c_cols = [], [], []
        for i in range(STEP):
            lv = r[i]
            bv = inv_ref[pl.ds(j + i, 1), :]
            cv = jnp.sum(jnp.where(cols == j + i, a_mat, 0.0), axis=1, keepdims=True)
            for k in range(i):
                lv = lv - low[i, k] * l_rows[k]
                bv = bv - low[i, k] * b_rows[k]
                cv = cv - low[i, k] * c_cols[k]
            l_rows.append(jnp.where(lane >= j + i, lv * inv[i], 0.0))
            b_rows.append(bv * inv[i])
            c_cols.append(cv * inv[i])
        new_a = a_mat
        new_b = inv_ref[...]
        for i in range(STEP):
            c = jnp.where(below, c_cols[i], 0.0)
            new_a = new_a - c * l_rows[i]
            new_b = new_b - c * b_rows[i]
        lt_ref[...] = new_a
        inv_ref[...] = new_b
        for i in range(STEP):
            lt_ref[pl.ds(j + i, 1), :] = l_rows[i]
            inv_ref[pl.ds(j + i, 1), :] = b_rows[i]
        return carry

    lax.fori_loop(0, n // STEP, step, 0)


def chol_inv(g):
    n = g.shape[0]
    return pl.pallas_call(
        chol_inv_kernel,
        out_shape=(
            jax.ShapeDtypeStruct((n, n), jnp.float32),
            jax.ShapeDtypeStruct((n, n), jnp.float32),
        ),
        in_specs=[pl.BlockSpec(memory_space=pltpu.VMEM)],
        out_specs=(pl.BlockSpec(memory_space=pltpu.VMEM), pl.BlockSpec(memory_space=pltpu.VMEM)),
    )(g)


HALF_PI_HI = 1.5703125
HALF_PI_LO = 4.8382679e-04


def sin_cos(angle):
    turns = jnp.round(angle * (2.0 / math.pi))
    rest = (angle - turns * HALF_PI_HI) - turns * HALF_PI_LO
    quadrant = turns.astype(jnp.int32) & 3
    sq = rest * rest
    sine = rest + rest * sq * (-1.0 / 6 + sq * (1.0 / 120 + sq * (-1.0 / 5040 + sq * (1.0 / 362880))))
    cosine = 1.0 + sq * (-0.5 + sq * (1.0 / 24 + sq * (-1.0 / 720 + sq * (1.0 / 40320))))
    swap = (quadrant & 1) == 1
    sin_v = jnp.where(swap, cosine, sine)
    cos_v = jnp.where(swap, sine, cosine)
    sin_v = jnp.where(quadrant >= 2, -sin_v, sin_v)
    cos_v = jnp.where((quadrant == 1) | (quadrant == 2), -cos_v, cos_v)
    return sin_v, cos_v


def jacobian_planes(pixels, wave_scale, flux_level, codes, field_re, field_im):
    delta_u = pixels // FOCAL - FOCAL // 2
    delta_v = pixels % FOCAL - FOCAL // 2
    mirror = codes // (GRID * GRID)
    column_x = codes // GRID % GRID - GRID // 2
    column_y = codes % GRID - GRID // 2
    phase_int = delta_u[:, None] * column_x[None, :] + delta_v[:, None] * column_y[None, :]
    radius = (delta_u * delta_u + delta_v * delta_v).astype(jnp.float32)
    amplitude = flux_level * jnp.exp(-INFL_RATE * radius / (FOCAL * FOCAL))
    defocus = radius * (TWO_PI * DEFOCUS_RATE / (FOCAL * FOCAL)) / wave_scale
    phase_angle = mirror.astype(jnp.float32)[None, :] * defocus[
        :, None
    ] - TWO_PI / FOCAL * wave_scale * phase_int.astype(jnp.float32)
    sine_part, cosine = sin_cos(phase_angle)
    real_part = amplitude[:, None] * (field_re[None, :] * cosine - field_im[None, :] * sine_part)
    imag_part = amplitude[:, None] * (field_re[None, :] * sine_part + field_im[None, :] * cosine)
    return real_part.astype(jnp.bfloat16), imag_part.astype(jnp.bfloat16)


BLOCK = 64

def jac_kernel(pix_ref, code_ref, field_ref, scale_ref, flux_ref, omega_ref, jac_ref, sketch_ref):
    npix = pix_ref.shape[1]
    wave_scale = scale_ref[0]
    flux_level = flux_ref[0]
    pixels = pix_ref[...]
    delta_u = pixels // FOCAL - FOCAL // 2
    delta_v = pixels % FOCAL - FOCAL // 2
    radius = (delta_u * delta_u + delta_v * delta_v).astype(jnp.float32)
    amplitude = flux_level * jnp.exp(-INFL_RATE * radius / (FOCAL * FOCAL))
    defocus = radius * (TWO_PI * DEFOCUS_RATE / (FOCAL * FOCAL)) / wave_scale
    zero = jnp.zeros_like(radius)
    terms = jnp.concatenate(
        [delta_u.astype(jnp.float32), delta_v.astype(jnp.float32), amplitude, defocus, zero, zero, zero, zero], axis=0
    ).T
    codes = code_ref[...]
    mirror = (codes // (GRID * GRID)).astype(jnp.float32)
    col_x = (codes // GRID % GRID - GRID // 2).astype(jnp.float32)
    col_y = (codes % GRID - GRID // 2).astype(jnp.float32)
    e_re = field_ref[0:1, :]
    e_im = field_ref[1:2, :]
    rate = TWO_PI / FOCAL * wave_scale
    for b in range(npix // BLOCK):
        t = terms[b * BLOCK : (b + 1) * BLOCK]
        du, dv, amp, defo = t[:, 0:1], t[:, 1:2], t[:, 2:3], t[:, 3:4]
        phase = mirror * defo - rate * (du * col_x + dv * col_y)
        sine, cosine = sin_cos(phase)
        jac_ref[b * BLOCK : (b + 1) * BLOCK, :] = (amp * (e_re * cosine - e_im * sine)).astype(jnp.bfloat16)
        jac_ref[npix + b * BLOCK : npix + (b + 1) * BLOCK, :] = (amp * (e_re * sine + e_im * cosine)).astype(jnp.bfloat16)
    sketch_ref[...] = jnp.dot(jac_ref[...], omega_ref[...], preferred_element_type=jnp.float32)

def split2(t):
    hi = t.astype(jnp.bfloat16)
    lo = (t - hi.astype(jnp.float32)).astype(jnp.bfloat16)
    return jnp.concatenate([hi, lo], axis=1)

def jac_table_kernel(pix_ref, code_ref, field_ref, scale_ref, flux_ref, omega_ref, jac_ref, sketch_ref):
    npix = pix_ref.shape[1]
    nact = code_ref.shape[1]
    g = GRID
    wave_scale = scale_ref[0]
    flux_level = flux_ref[0]
    pixels = pix_ref[...]
    delta_u = pixels // FOCAL - FOCAL // 2
    delta_v = pixels % FOCAL - FOCAL // 2
    radius = (delta_u * delta_u + delta_v * delta_v).astype(jnp.float32)
    amplitude = flux_level * jnp.exp(-INFL_RATE * radius / (FOCAL * FOCAL))
    defocus = radius * (TWO_PI * DEFOCUS_RATE / (FOCAL * FOCAL)) / wave_scale
    zero = jnp.zeros_like(radius)
    terms = jnp.concatenate(
        [delta_u.astype(jnp.float32), delta_v.astype(jnp.float32), amplitude, defocus, zero, zero, zero, zero], axis=0
    ).T
    du, dv, amp, defo = terms[:, 0:1], terms[:, 1:2], terms[:, 2:3], terms[:, 3:4]
    rate = TWO_PI / FOCAL * wave_scale
    offs = (lax.broadcasted_iota(jnp.int32, (1, g), 1) - g // 2).astype(jnp.float32)
    su, cu = sin_cos(-rate * (du * offs))
    sv, cv = sin_cos(-rate * (dv * offs))
    sf, cf = sin_cos(defo)
    ure = jnp.concatenate([cu, cu * cf - su * sf], axis=1)
    uim = jnp.concatenate([su, cu * sf + su * cf], axis=1)
    codes = code_ref[...]
    mirror = codes // (g * g)
    col_x = codes // g % g
    col_y = codes % g
    pick_x = lax.broadcasted_iota(jnp.int32, (2 * g, nact), 0) == mirror * g + col_x
    pick_y = lax.broadcasted_iota(jnp.int32, (g, nact), 0) == col_y
    ox = pick_x.astype(jnp.bfloat16)
    oy = pick_y.astype(jnp.bfloat16)
    ox2 = jnp.concatenate([ox, ox], axis=0)
    oy2 = jnp.concatenate([oy, oy], axis=0)
    f32 = jnp.float32
    tu_re, tu_im, tv_re, tv_im = split2(ure), split2(uim), split2(cv), split2(sv)
    e_re = field_ref[0:1, :]
    e_im = field_ref[1:2, :]
    rb = 128
    for b in range(npix // rb):
        sl = slice(b * rb, (b + 1) * rb)
        u_re = jnp.dot(tu_re[sl], ox2, preferred_element_type=f32)
        u_im = jnp.dot(tu_im[sl], ox2, preferred_element_type=f32)
        v_re = jnp.dot(tv_re[sl], oy2, preferred_element_type=f32)
        v_im = jnp.dot(tv_im[sl], oy2, preferred_element_type=f32)
        w_re = u_re * v_re - u_im * v_im
        w_im = u_re * v_im + u_im * v_re
        a_b = amp[sl]
        jac_ref[b * rb : (b + 1) * rb, :] = (a_b * (e_re * w_re - e_im * w_im)).astype(jnp.bfloat16)
        jac_ref[npix + b * rb : npix + (b + 1) * rb, :] = (a_b * (e_re * w_im + e_im * w_re)).astype(jnp.bfloat16)
    sketch_ref[...] = jnp.dot(jac_ref[...], omega_ref[...], preferred_element_type=jnp.float32)


def jac_and_sketch(pixel_row, codes_row, field, scale, flux, omega):
    npix = pixel_row.shape[1]; nact = codes_row.shape[1]
    vm = pl.BlockSpec(memory_space=pltpu.VMEM)
    return pl.pallas_call(
        jac_table_kernel,
        out_shape=(jax.ShapeDtypeStruct((2 * npix, nact), jnp.bfloat16), jax.ShapeDtypeStruct((2 * npix, omega.shape[1]), jnp.float32)),
        in_specs=[vm, vm, vm, pl.BlockSpec(memory_space=pltpu.SMEM), pl.BlockSpec(memory_space=pltpu.SMEM), vm],
        out_specs=(vm, vm),
    )(pixel_row, codes_row, field, scale, flux, omega)


def gram_of(sketch):
    return lax.dot_general(
        sketch,
        sketch,
        (((0,), (0,)), ((), ())),
        precision=lax.Precision.HIGHEST,
        preferred_element_type=jnp.float32,
    )


def on_device(pixel_index, act_map, omega, pupil_field, channel_scale, channel_flux):
    pixels = pixel_index[0]
    npix = pixels.shape[0]
    rows_dev = 2 * npix
    act_count = lax.axis_size("act")
    pix_count = lax.axis_size("pix")
    total_rows = rows_dev * pix_count
    share_pix = npix // act_count
    jac, partial_sketch = jac_and_sketch(
        pixel_index, act_map[None, :], pupil_field[0], channel_scale, channel_flux, omega
    )
    sketch = sum_by_parts(partial_sketch, "act")
    gram_matrix = paired_sum(gram_of(sketch), "pix")
    upper_factor, lower_inverse = chol_inv(gram_matrix)
    basis = lax.dot_general(
        sketch,
        lower_inverse,
        (((1,), (1,)), ((), ())),
        precision=lax.Precision.HIGHEST,
        preferred_element_type=jnp.float32,
    )
    first = lax.axis_index("act") * share_pix
    own_re = lax.dynamic_slice_in_dim(basis, first, share_pix, 0)
    own_im = lax.dynamic_slice_in_dim(basis, npix + first, share_pix, 0)
    own_basis = jnp.stack([own_re, own_im], axis=1).reshape(2 * share_pix, RANK)
    coarse = basis.astype(jnp.bfloat16)
    partial_value = lax.dot_general(
        coarse, jac, (((0,), (0,)), ((), ())), preferred_element_type=jnp.float32
    )
    parts = in_blocks(partial_value.astype(jnp.bfloat16), 0, pix_count)
    arrived = lax.all_to_all(parts, "pix", split_axis=0, concat_axis=0, tiled=True)
    projection = arrived.astype(jnp.float32).sum(axis=0)
    basis_out = (own_basis * math.sqrt(total_rows)).reshape(1, 2 * share_pix, RANK)
    r_factor = upper_factor / math.sqrt(total_rows * ACT)
    return (basis_out, projection, r_factor)


def solution(mesh):
    return jax.shard_map(
        on_device,
        mesh=mesh,
        in_specs=(
            P("pix", None),
            P("act"),
            P("act", None),
            P("pix", None, "act"),
            P("pix"),
            P("pix"),
        ),
        out_specs=(P("pix", "act", None), P("pix", "act"), P()),
        check_vma=False,
    )
```

```python
import math

import jax
import jax.numpy as jnp
from jax import lax
from jax.experimental import pallas as pl
from jax.experimental.pallas import tpu as pltpu
from jax.sharding import PartitionSpec as P

GRID = 128
FOCAL = 256
RANK = 128
ACT = 32768


TWO_PI = 2.0 * math.pi
INFL_RATE = 4.5
DEFOCUS_RATE = 6.0


def rows_for(lines, count):
    spare = -len(lines) % count
    return jnp.pad(lines, [(0, spare)] + [(0, 0)] * (lines.ndim - 1))


def sent_to_all(value, axis):
    copies = jnp.broadcast_to(value, (lax.axis_size(axis), *value.shape))
    return lax.all_to_all(copies, axis, split_axis=0, concat_axis=0, tiled=True)


def laid_out(parts, dim):
    shape = list(parts.shape[1:])
    shape[dim] *= parts.shape[0]
    return jnp.moveaxis(parts, 0, dim).reshape(shape)


def collect(value, axis, dim):
    parts = sent_to_all(value, axis)
    return laid_out(parts, dim)


def in_blocks(value, dim, count):
    before, after = (value.shape[:dim], value.shape[dim + 1 :])
    return jnp.moveaxis(value.reshape(*before, count, -1, *after), dim, 0)


def summed_on_arrival(value, axis, dim):
    parts = in_blocks(value, dim, lax.axis_size(axis))
    arrived = lax.all_to_all(parts, axis, split_axis=0, concat_axis=0, tiled=True)
    return arrived.sum(axis=0)


def sum_by_parts(value, axes):
    lines = value.reshape(-1, value.shape[-1])
    padded = rows_for(lines, lax.axis_size(axes))
    whole = collect(summed_on_arrival(padded, axes, 0), axes, 0)
    return lax.slice_in_dim(whole, 0, len(lines)).reshape(value.shape)


def paired_sum(value, axis):
    count = lax.axis_size(axis)
    pair = value + lax.ppermute(value, axis, [(i, i ^ 1) for i in range(count)])
    pairs = count // 2
    got = [pair] + [
        lax.ppermute(pair, axis, [(i, i ^ (2 * m)) for i in range(count)]) for m in range(1, pairs)
    ]
    mine = lax.axis_index(axis) // 2
    total = None
    for q in range(pairs):
        term = sum(jnp.where((mine ^ m) == q, got[m], 0.0) for m in range(pairs))
        total = term if total is None else total + term
    return total


def butterfly_sum(value, axis):
    count = lax.axis_size(axis)
    step = 1
    while step < count:
        pairs = [(i, i ^ step) for i in range(count)]
        value = value + lax.ppermute(value, axis, pairs)
        step *= 2
    return value


STEP = 4


def chol_inv_kernel(g_ref, lt_ref, inv_ref):
    n = g_ref.shape[0]
    lt_ref[...] = g_ref[...]
    rows = lax.broadcasted_iota(jnp.int32, (n, n), 0)
    cols = lax.broadcasted_iota(jnp.int32, (n, n), 1)
    inv_ref[...] = jnp.where(rows == cols, 1.0, 0.0).astype(jnp.float32)
    lane = lax.broadcasted_iota(jnp.int32, (1, n), 1)
    sub = lax.broadcasted_iota(jnp.int32, (n, 1), 0)

    def step(t, carry):
        j = STEP * t
        a_mat = lt_ref[...]
        r = [lt_ref[pl.ds(j + i, 1), :] for i in range(STEP)]
        blk = {}
        for i in range(STEP):
            for k in range(i, STEP):
                blk[i, k] = jnp.sum(jnp.where(lane == j + k, r[i], 0.0), axis=1, keepdims=True)
        low, inv = {}, []
        for i in range(STEP):
            s = blk[i, i]
            for k in range(i):
                s = s - low[i, k] * low[i, k]
            inv.append(lax.rsqrt(s))
            for m in range(i + 1, STEP):
                v = blk[i, m]
                for k in range(i):
                    v = v - low[m, k] * low[i, k]
                low[m, i] = v * inv[i]
        below = sub >= j + STEP
        l_rows, b_rows, c_cols = [], [], []
        for i in range(STEP):
            lv = r[i]
            bv = inv_ref[pl.ds(j + i, 1), :]
            cv = jnp.sum(jnp.where(cols == j + i, a_mat, 0.0), axis=1, keepdims=True)
            for k in range(i):
                lv = lv - low[i, k] * l_rows[k]
                bv = bv - low[i, k] * b_rows[k]
                cv = cv - low[i, k] * c_cols[k]
            l_rows.append(jnp.where(lane >= j + i, lv * inv[i], 0.0))
            b_rows.append(bv * inv[i])
            c_cols.append(cv * inv[i])
        new_a = a_mat
        new_b = inv_ref[...]
        for i in range(STEP):
            c = jnp.where(below, c_cols[i], 0.0)
            new_a = new_a - c * l_rows[i]
            new_b = new_b - c * b_rows[i]
        lt_ref[...] = new_a
        inv_ref[...] = new_b
        for i in range(STEP):
            lt_ref[pl.ds(j + i, 1), :] = l_rows[i]
            inv_ref[pl.ds(j + i, 1), :] = b_rows[i]
        return carry

    lax.fori_loop(0, n // STEP, step, 0)


def chol_inv(g):
    n = g.shape[0]
    return pl.pallas_call(
        chol_inv_kernel,
        out_shape=(
            jax.ShapeDtypeStruct((n, n), jnp.float32),
            jax.ShapeDtypeStruct((n, n), jnp.float32),
        ),
        in_specs=[pl.BlockSpec(memory_space=pltpu.VMEM)],
        out_specs=(pl.BlockSpec(memory_space=pltpu.VMEM), pl.BlockSpec(memory_space=pltpu.VMEM)),
    )(g)


HALF_PI_HI = 1.5703125
HALF_PI_LO = 4.8382679e-04


def sin_cos(angle):
    turns = jnp.round(angle * (2.0 / math.pi))
    rest = (angle - turns * HALF_PI_HI) - turns * HALF_PI_LO
    quadrant = turns.astype(jnp.int32) & 3
    sq = rest * rest
    sine = rest + rest * sq * (-1.0 / 6 + sq * (1.0 / 120 + sq * (-1.0 / 5040)))
    cosine = 1.0 + sq * (-0.5 + sq * (1.0 / 24 + sq * (-1.0 / 720)))
    swap = (quadrant & 1) == 1
    sin_v = jnp.where(swap, cosine, sine)
    cos_v = jnp.where(swap, sine, cosine)
    sin_v = jnp.where(quadrant >= 2, -sin_v, sin_v)
    cos_v = jnp.where((quadrant == 1) | (quadrant == 2), -cos_v, cos_v)
    return sin_v, cos_v


def jacobian_planes(pixels, wave_scale, flux_level, codes, field_re, field_im):
    delta_u = pixels // FOCAL - FOCAL // 2
    delta_v = pixels % FOCAL - FOCAL // 2
    mirror = codes // (GRID * GRID)
    column_x = codes // GRID % GRID - GRID // 2
    column_y = codes % GRID - GRID // 2
    phase_int = delta_u[:, None] * column_x[None, :] + delta_v[:, None] * column_y[None, :]
    radius = (delta_u * delta_u + delta_v * delta_v).astype(jnp.float32)
    amplitude = flux_level * jnp.exp(-INFL_RATE * radius / (FOCAL * FOCAL))
    defocus = radius * (TWO_PI * DEFOCUS_RATE / (FOCAL * FOCAL)) / wave_scale
    phase_angle = mirror.astype(jnp.float32)[None, :] * defocus[
        :, None
    ] - TWO_PI / FOCAL * wave_scale * phase_int.astype(jnp.float32)
    sine_part, cosine = sin_cos(phase_angle)
    real_part = amplitude[:, None] * (field_re[None, :] * cosine - field_im[None, :] * sine_part)
    imag_part = amplitude[:, None] * (field_re[None, :] * sine_part + field_im[None, :] * cosine)
    return real_part.astype(jnp.bfloat16), imag_part.astype(jnp.bfloat16)


BLOCK = 64

def jac_kernel(pix_ref, code_ref, field_ref, scale_ref, flux_ref, omega_ref, jac_ref, sketch_ref):
    npix = pix_ref.shape[1]
    wave_scale = scale_ref[0]
    flux_level = flux_ref[0]
    pixels = pix_ref[...]
    delta_u = pixels // FOCAL - FOCAL // 2
    delta_v = pixels % FOCAL - FOCAL // 2
    radius = (delta_u * delta_u + delta_v * delta_v).astype(jnp.float32)
    amplitude = flux_level * jnp.exp(-INFL_RATE * radius / (FOCAL * FOCAL))
    defocus = radius * (TWO_PI * DEFOCUS_RATE / (FOCAL * FOCAL)) / wave_scale
    zero = jnp.zeros_like(radius)
    terms = jnp.concatenate(
        [delta_u.astype(jnp.float32), delta_v.astype(jnp.float32), amplitude, defocus, zero, zero, zero, zero], axis=0
    ).T
    codes = code_ref[...]
    mirror = (codes // (GRID * GRID)).astype(jnp.float32)
    col_x = (codes // GRID % GRID - GRID // 2).astype(jnp.float32)
    col_y = (codes % GRID - GRID // 2).astype(jnp.float32)
    e_re = field_ref[0:1, :]
    e_im = field_ref[1:2, :]
    rate = TWO_PI / FOCAL * wave_scale
    for b in range(npix // BLOCK):
        t = terms[b * BLOCK : (b + 1) * BLOCK]
        du, dv, amp, defo = t[:, 0:1], t[:, 1:2], t[:, 2:3], t[:, 3:4]
        phase = mirror * defo - rate * (du * col_x + dv * col_y)
        sine, cosine = sin_cos(phase)
        jac_ref[b * BLOCK : (b + 1) * BLOCK, :] = (amp * (e_re * cosine - e_im * sine)).astype(jnp.bfloat16)
        jac_ref[npix + b * BLOCK : npix + (b + 1) * BLOCK, :] = (amp * (e_re * sine + e_im * cosine)).astype(jnp.bfloat16)
    sketch_ref[...] = jnp.dot(jac_ref[...], omega_ref[...], preferred_element_type=jnp.float32)

def jac_and_sketch(pixel_row, codes_row, field, scale, flux, omega):
    npix = pixel_row.shape[1]; nact = codes_row.shape[1]
    vm = pl.BlockSpec(memory_space=pltpu.VMEM)
    return pl.pallas_call(
        jac_kernel,
        out_shape=(jax.ShapeDtypeStruct((2 * npix, nact), jnp.bfloat16), jax.ShapeDtypeStruct((2 * npix, omega.shape[1]), jnp.float32)),
        in_specs=[vm, vm, vm, pl.BlockSpec(memory_space=pltpu.SMEM), pl.BlockSpec(memory_space=pltpu.SMEM), vm],
        out_specs=(vm, vm),
    )(pixel_row, codes_row, field, scale, flux, omega)


def gram_of(sketch):
    return lax.dot_general(
        sketch,
        sketch,
        (((0,), (0,)), ((), ())),
        precision=lax.Precision.HIGHEST,
        preferred_element_type=jnp.float32,
    )


def on_device(pixel_index, act_map, omega, pupil_field, channel_scale, channel_flux):
    pixels = pixel_index[0]
    npix = pixels.shape[0]
    rows_dev = 2 * npix
    act_count = lax.axis_size("act")
    pix_count = lax.axis_size("pix")
    total_rows = rows_dev * pix_count
    share_pix = npix // act_count
    jac, partial_sketch = jac_and_sketch(
        pixel_index, act_map[None, :], pupil_field[0], channel_scale, channel_flux, omega
    )
    sketch = sum_by_parts(partial_sketch, "act")
    gram_matrix = paired_sum(gram_of(sketch), "pix")
    upper_factor, lower_inverse = chol_inv(gram_matrix)
    basis = lax.dot_general(
        sketch,
        lower_inverse,
        (((1,), (1,)), ((), ())),
        precision=lax.Precision.HIGHEST,
        preferred_element_type=jnp.float32,
    )
    first = lax.axis_index("act") * share_pix
    own_re = lax.dynamic_slice_in_dim(basis, first, share_pix, 0)
    own_im = lax.dynamic_slice_in_dim(basis, npix + first, share_pix, 0)
    own_basis = jnp.stack([own_re, own_im], axis=1).reshape(2 * share_pix, RANK)
    coarse = basis.astype(jnp.bfloat16)
    partial_value = lax.dot_general(
        coarse, jac, (((0,), (0,)), ((), ())), preferred_element_type=jnp.float32
    )
    parts = in_blocks(partial_value.astype(jnp.bfloat16), 0, pix_count)
    arrived = lax.all_to_all(parts, "pix", split_axis=0, concat_axis=0, tiled=True)
    projection = arrived.astype(jnp.float32).sum(axis=0)
    basis_out = (own_basis * math.sqrt(total_rows)).reshape(1, 2 * share_pix, RANK)
    r_factor = upper_factor / math.sqrt(total_rows * ACT)
    return (basis_out, projection, r_factor)


def solution(mesh):
    return jax.shard_map(
        on_device,
        mesh=mesh,
        in_specs=(
            P("pix", None),
            P("act"),
            P("act", None),
            P("pix", None, "act"),
            P("pix"),
            P("pix"),
        ),
        out_specs=(P("pix", "act", None), P("pix", "act"), P()),
        check_vma=False,
    )
```

```python
import math

import jax
import jax.numpy as jnp
from jax import lax
from jax.experimental import pallas as pl
from jax.experimental.pallas import tpu as pltpu
from jax.sharding import PartitionSpec as P

GRID = 128
FOCAL = 256
RANK = 128
ACT = 32768


TWO_PI = 2.0 * math.pi
INFL_RATE = 4.5
DEFOCUS_RATE = 6.0


def rows_for(lines, count):
    spare = -len(lines) % count
    return jnp.pad(lines, [(0, spare)] + [(0, 0)] * (lines.ndim - 1))


def sent_to_all(value, axis):
    copies = jnp.broadcast_to(value, (lax.axis_size(axis), *value.shape))
    return lax.all_to_all(copies, axis, split_axis=0, concat_axis=0, tiled=True)


def laid_out(parts, dim):
    shape = list(parts.shape[1:])
    shape[dim] *= parts.shape[0]
    return jnp.moveaxis(parts, 0, dim).reshape(shape)


def collect(value, axis, dim):
    parts = sent_to_all(value, axis)
    return laid_out(parts, dim)


def in_blocks(value, dim, count):
    before, after = (value.shape[:dim], value.shape[dim + 1 :])
    return jnp.moveaxis(value.reshape(*before, count, -1, *after), dim, 0)


def summed_on_arrival(value, axis, dim):
    parts = in_blocks(value, dim, lax.axis_size(axis))
    arrived = lax.all_to_all(parts, axis, split_axis=0, concat_axis=0, tiled=True)
    return arrived.sum(axis=0)


def sum_by_parts(value, axes):
    lines = value.reshape(-1, value.shape[-1])
    padded = rows_for(lines, lax.axis_size(axes))
    whole = collect(summed_on_arrival(padded, axes, 0), axes, 0)
    return lax.slice_in_dim(whole, 0, len(lines)).reshape(value.shape)


def paired_sum(value, axis):
    count = lax.axis_size(axis)
    pair = value + lax.ppermute(value, axis, [(i, i ^ 1) for i in range(count)])
    pairs = count // 2
    got = [pair] + [
        lax.ppermute(pair, axis, [(i, i ^ (2 * m)) for i in range(count)]) for m in range(1, pairs)
    ]
    mine = lax.axis_index(axis) // 2
    total = None
    for q in range(pairs):
        term = sum(jnp.where((mine ^ m) == q, got[m], 0.0) for m in range(pairs))
        total = term if total is None else total + term
    return total


def butterfly_sum(value, axis):
    count = lax.axis_size(axis)
    step = 1
    while step < count:
        pairs = [(i, i ^ step) for i in range(count)]
        value = value + lax.ppermute(value, axis, pairs)
        step *= 2
    return value


STEP = 4


def chol_inv_kernel(g_ref, lt_ref, inv_ref):
    n = g_ref.shape[0]
    lt_ref[...] = g_ref[...]
    rows = lax.broadcasted_iota(jnp.int32, (n, n), 0)
    cols = lax.broadcasted_iota(jnp.int32, (n, n), 1)
    inv_ref[...] = jnp.where(rows == cols, 1.0, 0.0).astype(jnp.float32)
    lane = lax.broadcasted_iota(jnp.int32, (1, n), 1)
    sub = lax.broadcasted_iota(jnp.int32, (n, 1), 0)

    def step(t, carry):
        j = STEP * t
        a_mat = lt_ref[...]
        r = [lt_ref[pl.ds(j + i, 1), :] for i in range(STEP)]
        blk = {}
        for i in range(STEP):
            for k in range(i, STEP):
                blk[i, k] = jnp.sum(jnp.where(lane == j + k, r[i], 0.0), axis=1, keepdims=True)
        low, inv = {}, []
        for i in range(STEP):
            s = blk[i, i]
            for k in range(i):
                s = s - low[i, k] * low[i, k]
            inv.append(lax.rsqrt(s))
            for m in range(i + 1, STEP):
                v = blk[i, m]
                for k in range(i):
                    v = v - low[m, k] * low[i, k]
                low[m, i] = v * inv[i]
        below = sub >= j + STEP
        l_rows, b_rows, c_cols = [], [], []
        for i in range(STEP):
            lv = r[i]
            bv = inv_ref[pl.ds(j + i, 1), :]
            cv = jnp.sum(jnp.where(cols == j + i, a_mat, 0.0), axis=1, keepdims=True)
            for k in range(i):
                lv = lv - low[i, k] * l_rows[k]
                bv = bv - low[i, k] * b_rows[k]
                cv = cv - low[i, k] * c_cols[k]
            l_rows.append(jnp.where(lane >= j + i, lv * inv[i], 0.0))
            b_rows.append(bv * inv[i])
            c_cols.append(cv * inv[i])
        new_a = a_mat
        new_b = inv_ref[...]
        for i in range(STEP):
            c = jnp.where(below, c_cols[i], 0.0)
            new_a = new_a - c * l_rows[i]
            new_b = new_b - c * b_rows[i]
        lt_ref[...] = new_a
        inv_ref[...] = new_b
        for i in range(STEP):
            lt_ref[pl.ds(j + i, 1), :] = l_rows[i]
            inv_ref[pl.ds(j + i, 1), :] = b_rows[i]
        return carry

    lax.fori_loop(0, n // STEP, step, 0)


def chol_inv(g):
    n = g.shape[0]
    return pl.pallas_call(
        chol_inv_kernel,
        out_shape=(
            jax.ShapeDtypeStruct((n, n), jnp.float32),
            jax.ShapeDtypeStruct((n, n), jnp.float32),
        ),
        in_specs=[pl.BlockSpec(memory_space=pltpu.VMEM)],
        out_specs=(pl.BlockSpec(memory_space=pltpu.VMEM), pl.BlockSpec(memory_space=pltpu.VMEM)),
    )(g)


HALF_PI_HI = 1.5703125
HALF_PI_LO = 4.8382679e-04


def sin_cos(angle):
    turns = jnp.round(angle * (2.0 / math.pi))
    rest = (angle - turns * HALF_PI_HI) - turns * HALF_PI_LO
    quadrant = turns.astype(jnp.int32) & 3
    sq = rest * rest
    sine = rest + rest * sq * (-1.0 / 6 + sq * (1.0 / 120 + sq * (-1.0 / 5040 + sq * (1.0 / 362880))))
    cosine = 1.0 + sq * (-0.5 + sq * (1.0 / 24 + sq * (-1.0 / 720 + sq * (1.0 / 40320))))
    swap = (quadrant & 1) == 1
    sin_v = jnp.where(swap, cosine, sine)
    cos_v = jnp.where(swap, sine, cosine)
    sin_v = jnp.where(quadrant >= 2, -sin_v, sin_v)
    cos_v = jnp.where((quadrant == 1) | (quadrant == 2), -cos_v, cos_v)
    return sin_v, cos_v


def jacobian_planes(pixels, wave_scale, flux_level, codes, field_re, field_im):
    delta_u = pixels // FOCAL - FOCAL // 2
    delta_v = pixels % FOCAL - FOCAL // 2
    mirror = codes // (GRID * GRID)
    column_x = codes // GRID % GRID - GRID // 2
    column_y = codes % GRID - GRID // 2
    phase_int = delta_u[:, None] * column_x[None, :] + delta_v[:, None] * column_y[None, :]
    radius = (delta_u * delta_u + delta_v * delta_v).astype(jnp.float32)
    amplitude = flux_level * jnp.exp(-INFL_RATE * radius / (FOCAL * FOCAL))
    defocus = radius * (TWO_PI * DEFOCUS_RATE / (FOCAL * FOCAL)) / wave_scale
    phase_angle = mirror.astype(jnp.float32)[None, :] * defocus[
        :, None
    ] - TWO_PI / FOCAL * wave_scale * phase_int.astype(jnp.float32)
    sine_part, cosine = sin_cos(phase_angle)
    real_part = amplitude[:, None] * (field_re[None, :] * cosine - field_im[None, :] * sine_part)
    imag_part = amplitude[:, None] * (field_re[None, :] * sine_part + field_im[None, :] * cosine)
    return real_part.astype(jnp.bfloat16), imag_part.astype(jnp.bfloat16)


BLOCK = 64

def jac_kernel(pix_ref, code_ref, field_ref, scale_ref, flux_ref, omega_ref, jac_ref, sketch_ref):
    npix = pix_ref.shape[1]
    wave_scale = scale_ref[0]
    flux_level = flux_ref[0]
    pixels = pix_ref[...]
    delta_u = pixels // FOCAL - FOCAL // 2
    delta_v = pixels % FOCAL - FOCAL // 2
    radius = (delta_u * delta_u + delta_v * delta_v).astype(jnp.float32)
    amplitude = flux_level * jnp.exp(-INFL_RATE * radius / (FOCAL * FOCAL))
    defocus = radius * (TWO_PI * DEFOCUS_RATE / (FOCAL * FOCAL)) / wave_scale
    zero = jnp.zeros_like(radius)
    terms = jnp.concatenate(
        [delta_u.astype(jnp.float32), delta_v.astype(jnp.float32), amplitude, defocus, zero, zero, zero, zero], axis=0
    ).T
    codes = code_ref[...]
    mirror = (codes // (GRID * GRID)).astype(jnp.float32)
    col_x = (codes // GRID % GRID - GRID // 2).astype(jnp.float32)
    col_y = (codes % GRID - GRID // 2).astype(jnp.float32)
    e_re = field_ref[0:1, :]
    e_im = field_ref[1:2, :]
    rate = TWO_PI / FOCAL * wave_scale
    for b in range(npix // BLOCK):
        t = terms[b * BLOCK : (b + 1) * BLOCK]
        du, dv, amp, defo = t[:, 0:1], t[:, 1:2], t[:, 2:3], t[:, 3:4]
        phase = mirror * defo - rate * (du * col_x + dv * col_y)
        sine, cosine = sin_cos(phase)
        jac_ref[b * BLOCK : (b + 1) * BLOCK, :] = (amp * (e_re * cosine - e_im * sine)).astype(jnp.bfloat16)
        jac_ref[npix + b * BLOCK : npix + (b + 1) * BLOCK, :] = (amp * (e_re * sine + e_im * cosine)).astype(jnp.bfloat16)
    sketch_ref[...] = jnp.dot(jac_ref[...], omega_ref[...], preferred_element_type=jnp.float32)

def jac_and_sketch(pixel_row, codes_row, field, scale, flux, omega):
    npix = pixel_row.shape[1]; nact = codes_row.shape[1]
    vm = pl.BlockSpec(memory_space=pltpu.VMEM)
    return pl.pallas_call(
        jac_kernel,
        out_shape=(jax.ShapeDtypeStruct((2 * npix, nact), jnp.bfloat16), jax.ShapeDtypeStruct((2 * npix, omega.shape[1]), jnp.float32)),
        in_specs=[vm, vm, vm, pl.BlockSpec(memory_space=pltpu.SMEM), pl.BlockSpec(memory_space=pltpu.SMEM), vm],
        out_specs=(vm, vm),
    )(pixel_row, codes_row, field, scale, flux, omega)


def gram_of(sketch):
    return lax.dot_general(
        sketch,
        sketch,
        (((0,), (0,)), ((), ())),
        precision=lax.Precision.HIGHEST,
        preferred_element_type=jnp.float32,
    )


def on_device(pixel_index, act_map, omega, pupil_field, channel_scale, channel_flux):
    pixels = pixel_index[0]
    npix = pixels.shape[0]
    rows_dev = 2 * npix
    act_count = lax.axis_size("act")
    pix_count = lax.axis_size("pix")
    total_rows = rows_dev * pix_count
    share_pix = npix // act_count
    jac, partial_sketch = jac_and_sketch(
        pixel_index, act_map[None, :], pupil_field[0], channel_scale, channel_flux, omega
    )
    sketch = sum_by_parts(partial_sketch, "act")
    gram_matrix = paired_sum(gram_of(sketch), "pix")
    upper_factor, lower_inverse = chol_inv(gram_matrix)
    basis = lax.dot_general(
        sketch,
        lower_inverse,
        (((1,), (1,)), ((), ())),
        precision=lax.Precision.HIGH,
        preferred_element_type=jnp.float32,
    )
    first = lax.axis_index("act") * share_pix
    own_re = lax.dynamic_slice_in_dim(basis, first, share_pix, 0)
    own_im = lax.dynamic_slice_in_dim(basis, npix + first, share_pix, 0)
    own_basis = jnp.stack([own_re, own_im], axis=1).reshape(2 * share_pix, RANK)
    coarse = basis.astype(jnp.bfloat16)
    partial_value = lax.dot_general(
        coarse, jac, (((0,), (0,)), ((), ())), preferred_element_type=jnp.float32
    )
    parts = in_blocks(partial_value.astype(jnp.bfloat16), 0, pix_count)
    arrived = lax.all_to_all(parts, "pix", split_axis=0, concat_axis=0, tiled=True)
    projection = arrived.astype(jnp.float32).sum(axis=0)
    basis_out = (own_basis * math.sqrt(total_rows)).reshape(1, 2 * share_pix, RANK)
    r_factor = upper_factor / math.sqrt(total_rows * ACT)
    return (basis_out, projection, r_factor)


def solution(mesh):
    return jax.shard_map(
        on_device,
        mesh=mesh,
        in_specs=(
            P("pix", None),
            P("act"),
            P("act", None),
            P("pix", None, "act"),
            P("pix"),
            P("pix"),
        ),
        out_specs=(P("pix", "act", None), P("pix", "act"), P()),
        check_vma=False,
    )
```
